32 devices in a mesh: grp: 4 (over y, x), feat: 8 (over z, core).
Axes of the slice: x: 2, y: 2, z: 4, core: 2. Of those that a mesh axis runs over, the one named last changes fastest.
Arguments:
- inputs: bfloat16 [32, 32, 2048], P(None, 'feat'), may hold values from -8 to 8
- labels: int32 [32], replicated, may hold values from 0 to 32767
- phases: float32 [32, 32, 1024], P('feat'), may hold values from -3.140625 to 3.140625
- sign_bits: int32 [8, 32, 32, 1024], P('grp', 'feat'), may hold values from 0 to 1
- moment_first: float32 [32, 32, 1024], P('feat', 'grp'), may hold values from -1.2 to 1.2
- moment_second: float32 [32, 32, 1024], P('feat', 'grp'), may hold values from 0.001 to 0.03
Outputs:
- estimate: float32 [32, 32, 1024], P('feat', 'grp')
- moment_first_new: float32 [32, 32, 1024], P('feat', 'grp')
- moment_second_new: float32 [32, 32, 1024], P('feat', 'grp')
- phases_next: float32 [32, 32, 1024], P('feat')
The draws below stay inside these ranges and needn't reach their ends.
All inputs are finite; a program needn't handle non-finite values.
Results may differ from the reference program's by a relative error of at most 0.00135.
The reference program's roundings to bfloat16 on the way count: a program that leaves them out, or rounds other values in their place, can miss the bound.
Values may be sent and summed in bfloat16 or wider, within the bound.
No kernel may reach another device: no remote copies, remote signals or barrier semaphores. Data moves between devices by JAX's collectives and lax.ppermute only.
A program may use at most 128 MiB of HBM per device.

```python
import math
import jax
import jax.numpy as jnp
import numpy as np
from jax import lax

BS = 1024
NB = 32
ROWS = 32
ADAM_STEP = 10
PAIRS = 8


def draw_inputs(key, part):
    full_shape = (ROWS, NB, 2 * BS)
    values = jnp.clip(jax.random.normal(key, full_shape, jnp.float32), -5.0, 5.0) * 0.7071
    return values.astype(jnp.bfloat16)


def place_ends(drawn, rng, smallest, high):
    place = [jax.random.randint(jax.random.fold_in(rng, axis), (), 0, length) for axis, length in enumerate(drawn.shape)]
    main_axis = drawn.shape.index(max(drawn.shape))
    next_to = place[:main_axis] + [(place[main_axis] + 1) % drawn.shape[main_axis]] + place[main_axis + 1:]
    return drawn.at[tuple(place)].set(smallest).at[tuple(next_to)].set(high)


def level_of(stream_key, extent, cuts, least, top_value):
    gain = 1.0
    for position, parts in cuts:
        heights = jax.random.uniform(jax.random.fold_in(jax.random.fold_in(stream_key, 6), position), (parts,), jnp.float32, least / len(cuts), top_value / len(cuts))
        gain = gain * jnp.repeat(jnp.exp(heights), extent[position] // parts).reshape((-1,) + (1,) * (len(extent) - 1 - position))
    return gain


def rank_table(number_of, lean):
    loads = [(1 << 20) // math.isqrt(grade ** lean) + 1 for grade in range(1, number_of + 1)]
    spread = 1 + sum(loads) // (1 << 30)
    return np.cumsum(np.array([max(1, weight // spread) for weight in loads]))


def skewed_ids(rng, extent, amount, skew):
    listing = rank_table(amount, skew)
    ticket = jax.random.randint(jax.random.fold_in(rng, 1), extent, 0, int(listing[amount - 1]))
    grade = jnp.searchsorted(jnp.asarray(listing, jnp.int32), ticket, side="right")
    return jax.random.permutation(jax.random.fold_in(rng, 2), amount)[grade].astype(jnp.int32)


def gaussian(own_key, extent, width, limit, cuts=(), kind=jnp.bfloat16):
    entries = jax.random.normal(own_key, extent, jnp.float32) * width
    if len(cuts) > 0:
        entries = level_of(own_key, extent, cuts, -0.22, 0.18) * entries
    return jnp.clip(entries, min=-limit, max=limit).astype(kind)


def setup_inputs(seed: int = 0) -> dict:
    splits = jax.random.split(jax.random.key(seed), 7)
    return {
        "inputs": draw_inputs(jax.random.fold_in(splits[6], 71), 0),
        "labels": place_ends(skewed_ids(splits[1], (ROWS,), NB * BS, 2), jax.random.fold_in(splits[1], 3), 0, (NB * BS) - 1).astype(jnp.int32),
        "phases": jnp.clip(jax.random.uniform(splits[2], (NB, NB, BS), jnp.float32, -3.140625, 3.140625), -3.140625, 3.140625),
        "sign_bits": place_ends(jax.random.randint(splits[3], (PAIRS, NB, NB, BS), 0, 2), jax.random.fold_in(splits[3], 1), 0, 1).astype(jnp.int32),
        "moment_first": gaussian(splits[4], (NB, NB, BS), 0.2, 1.2, ((0, 8), (1, 4)), jnp.float32),
        "moment_second": jnp.clip(jnp.exp(math.log(0.03) - 3.4011973 * jax.random.uniform(splits[5], (NB, NB, BS), jnp.float32) ** level_of(splits[5], (NB, NB, BS), ((0, 8), (1, 4)), -0.2, 0.2)), 0.001, 0.03),
    }


logit_scale = 3.0
perturb_size = 0.2
learn_rate = 0.1
beta_first = 0.9
beta_second = 0.999
adam_eps = 1e-08

def tables(block_len):
    counter = jnp.arange(block_len, dtype=jnp.int32)
    product = counter[:, None] * counter[None, :] % block_len
    angles = product.astype(jnp.float32) * (2.0 * math.pi / block_len)
    factor = 1.0 / math.sqrt(block_len)
    cosine = (jnp.cos(angles) * factor).astype(jnp.bfloat16)
    sine_part = (jnp.sin(angles) * factor).astype(jnp.bfloat16)
    forward = jnp.concatenate([jnp.concatenate([cosine, -sine_part], 1), jnp.concatenate([sine_part, cosine], 1)], 0)
    inverse = jnp.concatenate([jnp.concatenate([cosine, sine_part], 1), jnp.concatenate([-sine_part, cosine], 1)], 0)
    return (forward, inverse)

def reference(inputs, labels, phases, sign_bits, moment_first, moment_second):
    forward, inverse = tables(BS)
    spectra = jnp.dot(inputs.reshape(ROWS * NB, 2 * BS), forward, preferred_element_type=jnp.float32)
    spectra = spectra.astype(jnp.bfloat16).reshape(ROWS, NB, 2 * BS)
    spec_real = spectra[..., :BS].astype(jnp.float32)
    spec_imag = spectra[..., BS:].astype(jnp.float32)
    classes = jnp.arange(NB * BS, dtype=jnp.int32)

    def net_loss(pair_bits, direction_sign):
        angles = phases + direction_sign * perturb_size * (2.0 * pair_bits.astype(jnp.float32) - 1.0)
        trans_real = lax.optimization_barrier(jnp.cos(angles).astype(jnp.bfloat16)).astype(jnp.float32)
        trans_imag = lax.optimization_barrier(jnp.sin(angles).astype(jnp.bfloat16)).astype(jnp.float32)
        mixed_real = jnp.einsum('ijk,rjk->rik', trans_real, spec_real) - jnp.einsum('ijk,rjk->rik', trans_imag, spec_imag)
        mixed_imag = jnp.einsum('ijk,rjk->rik', trans_real, spec_imag) + jnp.einsum('ijk,rjk->rik', trans_imag, spec_real)
        mixed = (jnp.concatenate([mixed_real, mixed_imag], -1) * (1.0 / math.sqrt(NB))).astype(jnp.bfloat16)
        output_field = jnp.dot(mixed.reshape(ROWS * NB, 2 * BS), inverse, preferred_element_type=jnp.float32)
        intensity = output_field[:, :BS] ** 2 + output_field[:, BS:] ** 2
        logits = logit_scale * intensity.reshape(ROWS, NB * BS)
        row_top = lax.optimization_barrier(jnp.max(logits, axis=1))
        row_total = lax.optimization_barrier(jnp.sum(jnp.exp(logits - row_top[:, None]), axis=1))
        row_label = lax.optimization_barrier(jnp.sum(jnp.where(classes[None, :] == labels[:, None], logits, 0.0), axis=1))
        return jnp.mean(row_top + jnp.log(row_total) - row_label)

    def pair_difference(pair_bits):
        return (net_loss(pair_bits, 1.0) - net_loss(pair_bits, -1.0)) / (2.0 * perturb_size)
    differences = lax.map(pair_difference, sign_bits)
    directions = 2.0 * sign_bits.astype(jnp.float32) - 1.0
    estimate = jnp.tensordot(differences, directions, 1, precision=lax.Precision.HIGHEST) / PAIRS
    first_new = beta_first * moment_first + (1.0 - beta_first) * estimate
    second_new = beta_second * moment_second + (1.0 - beta_second) * estimate * estimate
    first_bias = 1.0 - beta_first ** ADAM_STEP
    second_bias = 1.0 - beta_second ** ADAM_STEP
    phases_next = phases - learn_rate * (first_new / first_bias) / (jnp.sqrt(second_new / second_bias) + adam_eps)
    return (estimate, first_new, second_new, phases_next)
```

```python
import functools
import math

import jax
import jax.numpy as jnp
from jax import lax
from jax.experimental import pallas as pl
from jax.experimental.pallas import tpu as pltpu
from jax.sharding import PartitionSpec as P

ADAM_STEP = 10


logit_scale = 3.0
perturb_size = 0.2
learn_rate = 0.1
beta_first = 0.9
beta_second = 0.999
adam_eps = 1e-08


def tables(block_len):
    low_len = 1 << (int(math.log2(block_len)) // 2)
    high_len = block_len // low_len
    counter = jnp.arange(block_len, dtype=jnp.int32)
    high = jnp.arange(high_len, dtype=jnp.int32) * low_len
    low = jnp.arange(low_len, dtype=jnp.int32)
    step = 2.0 * math.pi / block_len
    high_angle = (high[:, None] * counter[None, :] % block_len).astype(jnp.float32) * step
    low_angle = (low[:, None] * counter[None, :] % block_len).astype(jnp.float32) * step
    high_cos, high_sin = jnp.cos(high_angle), jnp.sin(high_angle)
    low_cos, low_sin = jnp.cos(low_angle), jnp.sin(low_angle)
    factor = 1.0 / math.sqrt(block_len)
    cosine = high_cos[:, None] * low_cos[None] - high_sin[:, None] * low_sin[None]
    sine_part = high_sin[:, None] * low_cos[None] + high_cos[:, None] * low_sin[None]
    cosine = (cosine * factor).astype(jnp.bfloat16).reshape(block_len, block_len)
    sine_part = (sine_part * factor).astype(jnp.bfloat16).reshape(block_len, block_len)
    return cosine, sine_part


def to_bf16(values):
    return lax.reduce_precision(values, exponent_bits=8, mantissa_bits=7)


def mix_kernel(s_ref, tr_ref, ti_ref, o_ref, s32_ref, *, blocks, block_len, rows, chunk, factor):
    @pl.when((pl.program_id(0) == 0) & (pl.program_id(1) == 0))
    def _():
        def convert(j, carry):
            s32_ref[j] = s_ref[j].astype(jnp.float32)
            return carry

        lax.fori_loop(0, blocks, convert, 0)

    for start in range(0, block_len, chunk):
        def step(j, carry):
            acc_real, acc_imag = carry
            t_real = tr_ref[0, 0, pl.ds(j, 1), pl.ds(start, chunk)]
            t_imag = ti_ref[0, 0, pl.ds(j, 1), pl.ds(start, chunk)]
            s_real = s32_ref[j, :, pl.ds(start, chunk)]
            s_imag = s32_ref[j, :, pl.ds(block_len + start, chunk)]
            acc_real = acc_real + (t_real * s_real - t_imag * s_imag)
            acc_imag = acc_imag + (t_real * s_imag + t_imag * s_real)
            return acc_real, acc_imag

        zero = jnp.zeros((rows, chunk), jnp.float32)
        acc_real, acc_imag = lax.fori_loop(0, blocks, step, (zero, zero), unroll=4)
        o_ref[0, 0, :, pl.ds(start, chunk)] = (acc_real * factor).astype(o_ref.dtype)
        o_ref[0, 0, :, pl.ds(block_len + start, chunk)] = (acc_imag * factor).astype(o_ref.dtype)


def mix(spectra_all, t_real, t_imag):
    blocks, rows, doubled = spectra_all.shape
    block_len = doubled // 2
    nets, owned = t_real.shape[:2]
    kernel = functools.partial(
        mix_kernel,
        blocks=blocks,
        block_len=block_len,
        rows=rows,
        chunk=256,
        factor=1.0 / math.sqrt(blocks),
    )
    t_spec = pl.BlockSpec((1, 1, blocks, block_len), lambda n, i: (n, i, 0, 0))
    return pl.pallas_call(
        kernel,
        grid=(nets, owned),
        in_specs=[pl.BlockSpec((blocks, rows, doubled), lambda n, i: (0, 0, 0)), t_spec, t_spec],
        out_specs=pl.BlockSpec((1, 1, rows, doubled), lambda n, i: (n, i, 0, 0)),
        out_shape=jax.ShapeDtypeStruct((nets, owned, rows, doubled), jnp.bfloat16),
        scratch_shapes=[pltpu.VMEM((blocks, rows, doubled), jnp.float32)],
        compiler_params=pltpu.CompilerParams(
            dimension_semantics=("arbitrary", "arbitrary"), vmem_limit_bytes=48 * 1024 * 1024
        ),
    )(spectra_all, t_real, t_imag)


def body(inputs, labels, phases, sign_bits, moment_first, moment_second):
    row_count, owned_blocks, doubled = inputs.shape
    block_len = doubled // 2
    blocks = phases.shape[1]
    pairs_here = sign_bits.shape[0]
    group_count = lax.axis_size("grp")
    feat_count = lax.axis_size("feat")
    total_pairs = pairs_here * group_count
    net_count = 2 * pairs_here
    own_columns = blocks // group_count
    group_index = lax.axis_index("grp")
    feat_index = lax.axis_index("feat")

    directions = (2 * sign_bits - 1).astype(jnp.bfloat16)
    all_directions = lax.all_gather(directions, "grp", axis=0, tiled=True)
    all_first = lax.all_gather(moment_first, "grp", axis=1, tiled=True)
    all_second = lax.all_gather(moment_second, "grp", axis=1, tiled=True)

    cosine, sine_part = tables(block_len)
    local_in = jnp.transpose(inputs, (1, 0, 2)).reshape(owned_blocks * row_count, doubled)
    in_real = local_in[:, :block_len]
    in_imag = local_in[:, block_len:]
    f32 = jnp.float32
    spec_real = jnp.dot(in_real, cosine, preferred_element_type=f32) + jnp.dot(
        in_imag, sine_part, preferred_element_type=f32
    )
    spec_imag = jnp.dot(in_imag, cosine, preferred_element_type=f32) - jnp.dot(
        in_real, sine_part, preferred_element_type=f32
    )
    spectra = jnp.concatenate([spec_real, spec_imag], 1).astype(jnp.bfloat16)
    spectra = spectra.reshape(owned_blocks, row_count, doubled)
    spectra_all = lax.all_gather(spectra, "feat", axis=0, tiled=True)

    angle_plus = phases + jnp.float32(perturb_size)
    angle_minus = phases - jnp.float32(perturb_size)
    cos_plus = to_bf16(jnp.cos(angle_plus))
    sin_plus = to_bf16(jnp.sin(angle_plus))
    cos_minus = to_bf16(jnp.cos(angle_minus))
    sin_minus = to_bf16(jnp.sin(angle_minus))
    up = sign_bits == 1
    t_real = jnp.stack(
        [jnp.where(up, cos_plus, cos_minus), jnp.where(up, cos_minus, cos_plus)], 1
    ).reshape(net_count, owned_blocks, blocks, block_len)
    t_imag = jnp.stack(
        [jnp.where(up, sin_plus, sin_minus), jnp.where(up, sin_minus, sin_plus)], 1
    ).reshape(net_count, owned_blocks, blocks, block_len)

    mixed = mix(spectra_all, t_real, t_imag)
    mixed = mixed.reshape(net_count * owned_blocks * row_count, doubled)
    mix_real = mixed[:, :block_len]
    mix_imag = mixed[:, block_len:]
    field_real = jnp.dot(mix_real, cosine, preferred_element_type=f32) - jnp.dot(
        mix_imag, sine_part, preferred_element_type=f32
    )
    field_imag = jnp.dot(mix_real, sine_part, preferred_element_type=f32) + jnp.dot(
        mix_imag, cosine, preferred_element_type=f32
    )
    intensity = field_real**2 + field_imag**2
    logits = logit_scale * intensity.reshape(net_count, owned_blocks, row_count, block_len)
    first_class = feat_index * (owned_blocks * block_len)
    classes = first_class + jnp.arange(owned_blocks * block_len, dtype=jnp.int32).reshape(
        owned_blocks, 1, block_len
    )
    matches = classes == labels[None, :, None]
    local_top = jnp.max(logits, axis=(1, 3))
    local_total = jnp.sum(jnp.exp(logits - local_top[:, None, :, None]), axis=(1, 3))
    local_label = jnp.sum(jnp.where(matches[None], logits, 0.0), axis=(1, 3))
    stats = jnp.stack([local_top, local_total, local_label], 0)
    all_stats = lax.all_gather(stats, ("grp", "feat"), axis=0, tiled=False)
    all_stats = all_stats.reshape(group_count, feat_count, 3, net_count, row_count)
    part_top = all_stats[:, :, 0]
    row_top = jnp.max(part_top, axis=1)
    row_total = jnp.sum(all_stats[:, :, 1] * jnp.exp(part_top - row_top[:, None]), axis=1)
    row_label = jnp.sum(all_stats[:, :, 2], axis=1)
    losses = jnp.mean(row_top + jnp.log(row_total) - row_label, axis=2)
    losses = losses.reshape(total_pairs, 2)
    differences = (losses[:, 0] - losses[:, 1]) / (2.0 * perturb_size)

    estimate_all = (
        jnp.tensordot(
            differences, all_directions.astype(f32), 1, precision=lax.Precision.HIGHEST
        )
        / total_pairs
    )
    first_bias = 1.0 - beta_first**ADAM_STEP
    second_bias = 1.0 - beta_second**ADAM_STEP
    first_all = beta_first * all_first + (1.0 - beta_first) * estimate_all
    second_all = beta_second * all_second + (1.0 - beta_second) * estimate_all * estimate_all
    phases_next = phases - learn_rate * (first_all / first_bias) / (
        jnp.sqrt(second_all / second_bias) + adam_eps
    )
    first_column = group_index * own_columns
    estimate = lax.dynamic_slice_in_dim(estimate_all, first_column, own_columns, 1)
    first_new = beta_first * moment_first + (1.0 - beta_first) * estimate
    second_new = beta_second * moment_second + (1.0 - beta_second) * estimate * estimate
    return (estimate, first_new, second_new, phases_next)


def solution(mesh):
    return jax.shard_map(
        body,
        mesh=mesh,
        in_specs=(
            P(None, "feat", None),
            P(),
            P("feat", None, None),
            P("grp", "feat", None, None),
            P("feat", "grp", None),
            P("feat", "grp", None),
        ),
        out_specs=(
            P("feat", "grp", None),
            P("feat", "grp", None),
            P("feat", "grp", None),
            P("feat", None, None),
        ),
        check_vma=False,
    )
```

```python
import functools
import math

import jax
import jax.numpy as jnp
from jax import lax
from jax.experimental import pallas as pl
from jax.experimental.pallas import tpu as pltpu
from jax.sharding import PartitionSpec as P

ADAM_STEP = 10


logit_scale = 3.0
perturb_size = 0.2
learn_rate = 0.1
beta_first = 0.9
beta_second = 0.999
adam_eps = 1e-08


def tables(block_len):
    low_len = 1 << (int(math.log2(block_len)) // 2)
    high_len = block_len // low_len
    counter = jnp.arange(block_len, dtype=jnp.int32)
    high = jnp.arange(high_len, dtype=jnp.int32) * low_len
    low = jnp.arange(low_len, dtype=jnp.int32)
    step = 2.0 * math.pi / block_len
    high_angle = (high[:, None] * counter[None, :] % block_len).astype(jnp.float32) * step
    low_angle = (low[:, None] * counter[None, :] % block_len).astype(jnp.float32) * step
    high_cos, high_sin = jnp.cos(high_angle), jnp.sin(high_angle)
    low_cos, low_sin = jnp.cos(low_angle), jnp.sin(low_angle)
    factor = 1.0 / math.sqrt(block_len)
    cosine = high_cos[:, None] * low_cos[None] - high_sin[:, None] * low_sin[None]
    sine_part = high_sin[:, None] * low_cos[None] + high_cos[:, None] * low_sin[None]
    cosine = (cosine * factor).astype(jnp.bfloat16).reshape(block_len, block_len)
    sine_part = (sine_part * factor).astype(jnp.bfloat16).reshape(block_len, block_len)
    return cosine, sine_part


def to_bf16(values):
    return lax.reduce_precision(values, exponent_bits=8, mantissa_bits=7)


def mix_kernel(s_ref, tr_ref, ti_ref, o_ref, s32_ref, *, blocks, block_len, rows, chunk, factor):
    @pl.when((pl.program_id(0) == 0) & (pl.program_id(1) == 0))
    def _():
        def convert(j, carry):
            s32_ref[j] = s_ref[j].astype(jnp.float32)
            return carry

        lax.fori_loop(0, blocks, convert, 0)

    for start in range(0, block_len, chunk):
        def step(j, carry):
            acc_real, acc_imag = carry
            t_real = tr_ref[0, 0, pl.ds(j, 1), pl.ds(start, chunk)]
            t_imag = ti_ref[0, 0, pl.ds(j, 1), pl.ds(start, chunk)]
            s_real = s32_ref[j, :, pl.ds(start, chunk)]
            s_imag = s32_ref[j, :, pl.ds(block_len + start, chunk)]
            acc_real = acc_real + (t_real * s_real - t_imag * s_imag)
            acc_imag = acc_imag + (t_real * s_imag + t_imag * s_real)
            return acc_real, acc_imag

        zero = jnp.zeros((rows, chunk), jnp.float32)
        acc_real, acc_imag = lax.fori_loop(0, blocks, step, (zero, zero), unroll=4)
        o_ref[0, 0, :, pl.ds(start, chunk)] = (acc_real * factor).astype(o_ref.dtype)
        o_ref[0, 0, :, pl.ds(block_len + start, chunk)] = (acc_imag * factor).astype(o_ref.dtype)


def mix(spectra_all, t_real, t_imag):
    blocks, rows, doubled = spectra_all.shape
    block_len = doubled // 2
    nets, owned = t_real.shape[:2]
    kernel = functools.partial(
        mix_kernel,
        blocks=blocks,
        block_len=block_len,
        rows=rows,
        chunk=256,
        factor=1.0 / math.sqrt(blocks),
    )
    t_spec = pl.BlockSpec((1, 1, blocks, block_len), lambda n, i: (n, i, 0, 0))
    return pl.pallas_call(
        kernel,
        grid=(nets, owned),
        in_specs=[pl.BlockSpec((blocks, rows, doubled), lambda n, i: (0, 0, 0)), t_spec, t_spec],
        out_specs=pl.BlockSpec((1, 1, rows, doubled), lambda n, i: (n, i, 0, 0)),
        out_shape=jax.ShapeDtypeStruct((nets, owned, rows, doubled), jnp.bfloat16),
        scratch_shapes=[pltpu.VMEM((blocks, rows, doubled), jnp.float32)],
        compiler_params=pltpu.CompilerParams(
            dimension_semantics=("arbitrary", "arbitrary"), vmem_limit_bytes=48 * 1024 * 1024
        ),
    )(spectra_all, t_real, t_imag)


def body(inputs, labels, phases, sign_bits, moment_first, moment_second):
    row_count, owned_blocks, doubled = inputs.shape
    block_len = doubled // 2
    blocks = phases.shape[1]
    pairs_here = sign_bits.shape[0]
    group_count = lax.axis_size("grp")
    feat_count = lax.axis_size("feat")
    total_pairs = pairs_here * group_count
    net_count = 2 * pairs_here
    own_columns = blocks // group_count
    group_index = lax.axis_index("grp")
    feat_index = lax.axis_index("feat")

    directions = (2 * sign_bits - 1).astype(jnp.bfloat16)
    all_directions = lax.all_gather(directions, "grp", axis=0, tiled=True)
    moments = jnp.transpose(jnp.stack([moment_first, moment_second], 0), (2, 0, 1, 3))
    all_moments = lax.all_gather(moments, "grp", axis=0, tiled=True)
    all_moments = jnp.transpose(all_moments, (1, 2, 0, 3))
    all_first = all_moments[0]
    all_second = all_moments[1]

    cosine, sine_part = tables(block_len)
    local_in = jnp.transpose(inputs, (1, 0, 2)).reshape(owned_blocks * row_count, doubled)
    in_real = local_in[:, :block_len]
    in_imag = local_in[:, block_len:]
    f32 = jnp.float32
    spec_real = jnp.dot(in_real, cosine, preferred_element_type=f32) + jnp.dot(
        in_imag, sine_part, preferred_element_type=f32
    )
    spec_imag = jnp.dot(in_imag, cosine, preferred_element_type=f32) - jnp.dot(
        in_real, sine_part, preferred_element_type=f32
    )
    spectra = jnp.concatenate([spec_real, spec_imag], 1).astype(jnp.bfloat16)
    spectra = spectra.reshape(owned_blocks, row_count, doubled)
    spectra_all = lax.all_gather(spectra, "feat", axis=0, tiled=True)

    angle_plus = phases + jnp.float32(perturb_size)
    angle_minus = phases - jnp.float32(perturb_size)
    cos_plus = to_bf16(jnp.cos(angle_plus))
    sin_plus = to_bf16(jnp.sin(angle_plus))
    cos_minus = to_bf16(jnp.cos(angle_minus))
    sin_minus = to_bf16(jnp.sin(angle_minus))
    up = sign_bits == 1
    t_real = jnp.stack(
        [jnp.where(up, cos_plus, cos_minus), jnp.where(up, cos_minus, cos_plus)], 1
    ).reshape(net_count, owned_blocks, blocks, block_len)
    t_imag = jnp.stack(
        [jnp.where(up, sin_plus, sin_minus), jnp.where(up, sin_minus, sin_plus)], 1
    ).reshape(net_count, owned_blocks, blocks, block_len)

    mixed = mix(spectra_all, t_real, t_imag)
    mixed = mixed.reshape(net_count * owned_blocks * row_count, doubled)
    mix_real = mixed[:, :block_len]
    mix_imag = mixed[:, block_len:]
    field_real = jnp.dot(mix_real, cosine, preferred_element_type=f32) - jnp.dot(
        mix_imag, sine_part, preferred_element_type=f32
    )
    field_imag = jnp.dot(mix_real, sine_part, preferred_element_type=f32) + jnp.dot(
        mix_imag, cosine, preferred_element_type=f32
    )
    intensity = field_real**2 + field_imag**2
    logits = logit_scale * intensity.reshape(net_count, owned_blocks, row_count, block_len)
    first_class = feat_index * (owned_blocks * block_len)
    classes = first_class + jnp.arange(owned_blocks * block_len, dtype=jnp.int32).reshape(
        owned_blocks, 1, block_len
    )
    matches = classes == labels[None, :, None]
    local_top = jnp.max(logits, axis=(1, 3))
    local_total = jnp.sum(jnp.exp(logits - local_top[:, None, :, None]), axis=(1, 3))
    local_label = jnp.sum(jnp.where(matches[None], logits, 0.0), axis=(1, 3))
    stats = jnp.stack([local_top, local_total, local_label], 0)
    all_stats = lax.all_gather(stats, "feat", axis=0, tiled=False)
    part_top = all_stats[:, 0]
    row_top = jnp.max(part_top, axis=0)
    row_total = jnp.sum(all_stats[:, 1] * jnp.exp(part_top - row_top[None]), axis=0)
    row_label = jnp.sum(all_stats[:, 2], axis=0)
    losses = jnp.mean(row_top + jnp.log(row_total) - row_label, axis=1)
    losses = losses.reshape(pairs_here, 2)
    own_differences = (losses[:, 0] - losses[:, 1]) / (2.0 * perturb_size)
    differences = lax.all_gather(own_differences, "grp", axis=0, tiled=True)

    estimate_all = (
        jnp.tensordot(
            differences, all_directions.astype(f32), 1, precision=lax.Precision.HIGHEST
        )
        / total_pairs
    )
    first_bias = 1.0 - beta_first**ADAM_STEP
    second_bias = 1.0 - beta_second**ADAM_STEP
    first_all = beta_first * all_first + (1.0 - beta_first) * estimate_all
    second_all = beta_second * all_second + (1.0 - beta_second) * estimate_all * estimate_all
    phases_next = phases - learn_rate * (first_all / first_bias) / (
        jnp.sqrt(second_all / second_bias) + adam_eps
    )
    first_column = group_index * own_columns
    estimate = lax.dynamic_slice_in_dim(estimate_all, first_column, own_columns, 1)
    first_new = beta_first * moment_first + (1.0 - beta_first) * estimate
    second_new = beta_second * moment_second + (1.0 - beta_second) * estimate * estimate
    return (estimate, first_new, second_new, phases_next)


def solution(mesh):
    return jax.shard_map(
        body,
        mesh=mesh,
        in_specs=(
            P(None, "feat", None),
            P(),
            P("feat", None, None),
            P("grp", "feat", None, None),
            P("feat", "grp", None),
            P("feat", "grp", None),
        ),
        out_specs=(
            P("feat", "grp", None),
            P("feat", "grp", None),
            P("feat", "grp", None),
            P("feat", None, None),
        ),
        check_vma=False,
    )
```

```python
import functools
import math

import jax
import jax.numpy as jnp
from jax import lax
from jax.experimental import pallas as pl
from jax.experimental.pallas import tpu as pltpu
from jax.sharding import PartitionSpec as P

ADAM_STEP = 10


logit_scale = 3.0
perturb_size = 0.2
learn_rate = 0.1
beta_first = 0.9
beta_second = 0.999
adam_eps = 1e-08


def tables(block_len):
    low_len = 1 << (int(math.log2(block_len)) // 2)
    high_len = block_len // low_len
    counter = jnp.arange(block_len, dtype=jnp.int32)
    high = jnp.arange(high_len, dtype=jnp.int32) * low_len
    low = jnp.arange(low_len, dtype=jnp.int32)
    step = 2.0 * math.pi / block_len
    high_angle = (high[:, None] * counter[None, :] % block_len).astype(jnp.float32) * step
    low_angle = (low[:, None] * counter[None, :] % block_len).astype(jnp.float32) * step
    high_cos, high_sin = jnp.cos(high_angle), jnp.sin(high_angle)
    low_cos, low_sin = jnp.cos(low_angle), jnp.sin(low_angle)
    factor = 1.0 / math.sqrt(block_len)
    cosine = high_cos[:, None] * low_cos[None] - high_sin[:, None] * low_sin[None]
    sine_part = high_sin[:, None] * low_cos[None] + high_cos[:, None] * low_sin[None]
    cosine = (cosine * factor).astype(jnp.bfloat16).reshape(block_len, block_len)
    sine_part = (sine_part * factor).astype(jnp.bfloat16).reshape(block_len, block_len)
    return cosine, sine_part


def to_bf16(values):
    return lax.reduce_precision(values, exponent_bits=8, mantissa_bits=7)


def mix_kernel(s_ref, tr_ref, ti_ref, o_ref, s32_ref, *, blocks, block_len, rows, chunk, factor):
    @pl.when((pl.program_id(0) == 0) & (pl.program_id(1) == 0))
    def _():
        def convert(j, carry):
            s32_ref[j] = s_ref[j].astype(jnp.float32)
            return carry

        lax.fori_loop(0, blocks, convert, 0)

    for start in range(0, block_len, chunk):
        def step(j, carry):
            acc_real, acc_imag = carry
            t_real = tr_ref[0, 0, pl.ds(j, 1), pl.ds(start, chunk)]
            t_imag = ti_ref[0, 0, pl.ds(j, 1), pl.ds(start, chunk)]
            s_real = s32_ref[j, :, pl.ds(start, chunk)]
            s_imag = s32_ref[j, :, pl.ds(block_len + start, chunk)]
            acc_real = acc_real + (t_real * s_real - t_imag * s_imag)
            acc_imag = acc_imag + (t_real * s_imag + t_imag * s_real)
            return acc_real, acc_imag

        zero = jnp.zeros((rows, chunk), jnp.float32)
        acc_real, acc_imag = lax.fori_loop(0, blocks, step, (zero, zero), unroll=4)
        o_ref[0, 0, :, pl.ds(start, chunk)] = (acc_real * factor).astype(o_ref.dtype)
        o_ref[0, 0, :, pl.ds(block_len + start, chunk)] = (acc_imag * factor).astype(o_ref.dtype)


def mix(spectra_all, t_real, t_imag):
    blocks, rows, doubled = spectra_all.shape
    block_len = doubled // 2
    nets, owned = t_real.shape[:2]
    kernel = functools.partial(
        mix_kernel,
        blocks=blocks,
        block_len=block_len,
        rows=rows,
        chunk=256,
        factor=1.0 / math.sqrt(blocks),
    )
    t_spec = pl.BlockSpec((1, 1, blocks, block_len), lambda n, i: (n, i, 0, 0))
    return pl.pallas_call(
        kernel,
        grid=(nets, owned),
        in_specs=[pl.BlockSpec((blocks, rows, doubled), lambda n, i: (0, 0, 0)), t_spec, t_spec],
        out_specs=pl.BlockSpec((1, 1, rows, doubled), lambda n, i: (n, i, 0, 0)),
        out_shape=jax.ShapeDtypeStruct((nets, owned, rows, doubled), jnp.bfloat16),
        scratch_shapes=[pltpu.VMEM((blocks, rows, doubled), jnp.float32)],
        compiler_params=pltpu.CompilerParams(
            dimension_semantics=("arbitrary", "arbitrary"), vmem_limit_bytes=48 * 1024 * 1024
        ),
    )(spectra_all, t_real, t_imag)


def body(inputs, labels, phases, sign_bits, moment_first, moment_second):
    row_count, owned_blocks, doubled = inputs.shape
    block_len = doubled // 2
    blocks = phases.shape[1]
    pairs_here = sign_bits.shape[0]
    group_count = lax.axis_size("grp")
    outer_count = lax.axis_size("fz")
    core_count = lax.axis_size("fc")
    total_pairs = pairs_here * group_count
    net_count = 2 * pairs_here
    own_columns = blocks // group_count
    group_index = lax.axis_index("grp")
    feat_index = lax.axis_index("fz") * core_count + lax.axis_index("fc")

    directions = (2 * sign_bits - 1).astype(jnp.bfloat16)
    all_directions = lax.all_gather(directions, "grp", axis=0, tiled=True)
    moments = jnp.transpose(jnp.stack([moment_first, moment_second], 0), (2, 0, 1, 3))
    all_moments = lax.all_gather(moments, "grp", axis=0, tiled=True)
    all_moments = jnp.transpose(all_moments, (1, 2, 0, 3))
    all_first = all_moments[0]
    all_second = all_moments[1]

    cosine, sine_part = tables(block_len)
    local_in = jnp.transpose(inputs, (1, 0, 2)).reshape(owned_blocks * row_count, doubled)
    in_real = local_in[:, :block_len]
    in_imag = local_in[:, block_len:]
    f32 = jnp.float32
    spec_real = jnp.dot(in_real, cosine, preferred_element_type=f32) + jnp.dot(
        in_imag, sine_part, preferred_element_type=f32
    )
    spec_imag = jnp.dot(in_imag, cosine, preferred_element_type=f32) - jnp.dot(
        in_real, sine_part, preferred_element_type=f32
    )
    spectra = jnp.concatenate([spec_real, spec_imag], 1).astype(jnp.bfloat16)
    spectra = spectra.reshape(owned_blocks, row_count, doubled)
    spectra_all = lax.all_gather(spectra, "fz", axis=0, tiled=True)
    spectra_all = lax.all_gather(spectra_all, "fc", axis=0, tiled=True)

    def core_major(values):
        lead = values.shape[:-2]
        values = values.reshape(lead + (outer_count, core_count, owned_blocks, block_len))
        values = jnp.swapaxes(values, -3, -4)
        return values.reshape(lead + (blocks, block_len))

    phases_order = core_major(phases)
    angle_plus = phases_order + jnp.float32(perturb_size)
    angle_minus = phases_order - jnp.float32(perturb_size)
    cos_plus = to_bf16(jnp.cos(angle_plus))
    sin_plus = to_bf16(jnp.sin(angle_plus))
    cos_minus = to_bf16(jnp.cos(angle_minus))
    sin_minus = to_bf16(jnp.sin(angle_minus))
    up = core_major(sign_bits) == 1
    t_real = jnp.stack(
        [jnp.where(up, cos_plus, cos_minus), jnp.where(up, cos_minus, cos_plus)], 1
    ).reshape(net_count, owned_blocks, blocks, block_len)
    t_imag = jnp.stack(
        [jnp.where(up, sin_plus, sin_minus), jnp.where(up, sin_minus, sin_plus)], 1
    ).reshape(net_count, owned_blocks, blocks, block_len)

    mixed = mix(spectra_all, t_real, t_imag)
    mixed = mixed.reshape(net_count * owned_blocks * row_count, doubled)
    mix_real = mixed[:, :block_len]
    mix_imag = mixed[:, block_len:]
    field_real = jnp.dot(mix_real, cosine, preferred_element_type=f32) - jnp.dot(
        mix_imag, sine_part, preferred_element_type=f32
    )
    field_imag = jnp.dot(mix_real, sine_part, preferred_element_type=f32) + jnp.dot(
        mix_imag, cosine, preferred_element_type=f32
    )
    intensity = field_real**2 + field_imag**2
    logits = logit_scale * intensity.reshape(net_count, owned_blocks, row_count, block_len)
    first_class = feat_index * (owned_blocks * block_len)
    classes = first_class + jnp.arange(owned_blocks * block_len, dtype=jnp.int32).reshape(
        owned_blocks, 1, block_len
    )
    matches = classes == labels[None, :, None]
    local_top = jnp.max(logits, axis=(1, 3))
    local_total = jnp.sum(jnp.exp(logits - local_top[:, None, :, None]), axis=(1, 3))
    local_label = jnp.sum(jnp.where(matches[None], logits, 0.0), axis=(1, 3))
    stats = jnp.stack([local_top, local_total, local_label], 0)
    all_stats = lax.all_gather(stats, ("fz", "fc"), axis=0, tiled=False)
    part_top = all_stats[:, 0]
    row_top = jnp.max(part_top, axis=0)
    row_total = jnp.sum(all_stats[:, 1] * jnp.exp(part_top - row_top[None]), axis=0)
    row_label = jnp.sum(all_stats[:, 2], axis=0)
    losses = jnp.mean(row_top + jnp.log(row_total) - row_label, axis=1)
    losses = losses.reshape(pairs_here, 2)
    own_differences = (losses[:, 0] - losses[:, 1]) / (2.0 * perturb_size)
    differences = lax.all_gather(own_differences, "grp", axis=0, tiled=True)

    estimate_all = (
        jnp.tensordot(
            differences, all_directions.astype(f32), 1, precision=lax.Precision.HIGHEST
        )
        / total_pairs
    )
    first_bias = 1.0 - beta_first**ADAM_STEP
    second_bias = 1.0 - beta_second**ADAM_STEP
    first_all = beta_first * all_first + (1.0 - beta_first) * estimate_all
    second_all = beta_second * all_second + (1.0 - beta_second) * estimate_all * estimate_all
    phases_next = phases - learn_rate * (first_all / first_bias) / (
        jnp.sqrt(second_all / second_bias) + adam_eps
    )
    first_column = group_index * own_columns
    estimate = lax.dynamic_slice_in_dim(estimate_all, first_column, own_columns, 1)
    first_new = beta_first * moment_first + (1.0 - beta_first) * estimate
    second_new = beta_second * moment_second + (1.0 - beta_second) * estimate * estimate
    return (estimate, first_new, second_new, phases_next)


def solution(mesh):
    group_count = mesh.shape["grp"]
    feat_count = mesh.shape["feat"]
    core_count = 2 if feat_count % 2 == 0 else 1
    devices = mesh.devices.reshape(group_count, feat_count // core_count, core_count)
    split_mesh = jax.sharding.Mesh(devices, ("grp", "fz", "fc"))
    feat = ("fz", "fc")
    return jax.shard_map(
        body,
        mesh=split_mesh,
        in_specs=(
            P(None, feat, None),
            P(),
            P(feat, None, None),
            P("grp", feat, None, None),
            P(feat, "grp", None),
            P(feat, "grp", None),
        ),
        out_specs=(
            P(feat, "grp", None),
            P(feat, "grp", None),
            P(feat, "grp", None),
            P(feat, None, None),
        ),
        check_vma=False,
    )
```

```python
import functools
import math

import jax
import jax.numpy as jnp
from jax import lax
from jax.experimental import pallas as pl
from jax.experimental.pallas import tpu as pltpu
from jax.sharding import PartitionSpec as P

ADAM_STEP = 10


logit_scale = 3.0
perturb_size = 0.2
learn_rate = 0.1
beta_first = 0.9
beta_second = 0.999
adam_eps = 1e-08


def tables(block_len):
    low_len = 1 << (int(math.log2(block_len)) // 2)
    high_len = block_len // low_len
    counter = jnp.arange(block_len, dtype=jnp.int32)
    high = jnp.arange(high_len, dtype=jnp.int32) * low_len
    low = jnp.arange(low_len, dtype=jnp.int32)
    step = 2.0 * math.pi / block_len
    high_angle = (high[:, None] * counter[None, :] % block_len).astype(jnp.float32) * step
    low_angle = (low[:, None] * counter[None, :] % block_len).astype(jnp.float32) * step
    high_cos, high_sin = jnp.cos(high_angle), jnp.sin(high_angle)
    low_cos, low_sin = jnp.cos(low_angle), jnp.sin(low_angle)
    factor = 1.0 / math.sqrt(block_len)
    cosine = high_cos[:, None] * low_cos[None] - high_sin[:, None] * low_sin[None]
    sine_part = high_sin[:, None] * low_cos[None] + high_cos[:, None] * low_sin[None]
    cosine = (cosine * factor).astype(jnp.bfloat16).reshape(block_len, block_len)
    sine_part = (sine_part * factor).astype(jnp.bfloat16).reshape(block_len, block_len)
    return cosine, sine_part


def to_bf16(values):
    return lax.reduce_precision(values, exponent_bits=8, mantissa_bits=7)


def mix_kernel(s_ref, tr_ref, ti_ref, o_ref, s32_ref, *, blocks, block_len, rows, chunk, factor):
    @pl.when((pl.program_id(0) == 0) & (pl.program_id(1) == 0))
    def _():
        def convert(j, carry):
            s32_ref[j] = s_ref[j].astype(jnp.float32)
            return carry

        lax.fori_loop(0, blocks, convert, 0)

    for start in range(0, block_len, chunk):
        def step(j, carry):
            acc_real, acc_imag = carry
            t_real = tr_ref[0, 0, pl.ds(j, 1), pl.ds(start, chunk)]
            t_imag = ti_ref[0, 0, pl.ds(j, 1), pl.ds(start, chunk)]
            s_real = s32_ref[j, :, pl.ds(start, chunk)]
            s_imag = s32_ref[j, :, pl.ds(block_len + start, chunk)]
            acc_real = acc_real + (t_real * s_real - t_imag * s_imag)
            acc_imag = acc_imag + (t_real * s_imag + t_imag * s_real)
            return acc_real, acc_imag

        zero = jnp.zeros((rows, chunk), jnp.float32)
        acc_real, acc_imag = lax.fori_loop(0, blocks, step, (zero, zero), unroll=4)
        o_ref[0, 0, :, pl.ds(start, chunk)] = (acc_real * factor).astype(o_ref.dtype)
        o_ref[0, 0, :, pl.ds(block_len + start, chunk)] = (acc_imag * factor).astype(o_ref.dtype)


def mix(spectra_all, t_real, t_imag):
    blocks, rows, doubled = spectra_all.shape
    block_len = doubled // 2
    nets, owned = t_real.shape[:2]
    kernel = functools.partial(
        mix_kernel,
        blocks=blocks,
        block_len=block_len,
        rows=rows,
        chunk=256,
        factor=1.0 / math.sqrt(blocks),
    )
    t_spec = pl.BlockSpec((1, 1, blocks, block_len), lambda n, i: (n, i, 0, 0))
    return pl.pallas_call(
        kernel,
        grid=(nets, owned),
        in_specs=[pl.BlockSpec((blocks, rows, doubled), lambda n, i: (0, 0, 0)), t_spec, t_spec],
        out_specs=pl.BlockSpec((1, 1, rows, doubled), lambda n, i: (n, i, 0, 0)),
        out_shape=jax.ShapeDtypeStruct((nets, owned, rows, doubled), jnp.bfloat16),
        scratch_shapes=[pltpu.VMEM((blocks, rows, doubled), jnp.float32)],
        compiler_params=pltpu.CompilerParams(
            dimension_semantics=("arbitrary", "arbitrary"), vmem_limit_bytes=48 * 1024 * 1024
        ),
    )(spectra_all, t_real, t_imag)


def gather_by_permutes(values, axis_name, size, index):
    parts = [values] + [
        lax.ppermute(values, axis_name, [(i, (i + s) % size) for i in range(size)])
        for s in range(1, size)
    ]
    order = (index - jnp.arange(size)) % size
    return jnp.take(jnp.stack(parts, 0), order, axis=0)


def merge_stats(top, total, label, axis_name, size):
    if size & (size - 1):
        tops, totals, labels = lax.all_gather((top, total, label), axis_name)
        merged = jnp.max(tops, axis=0)
        merged_total = jnp.sum(totals * jnp.exp(tops - merged[None]), axis=0)
        return merged, merged_total, jnp.sum(labels, axis=0)
    step = 1
    while step < size:
        perm = [(i, i ^ step) for i in range(size)]
        packed = lax.ppermute(jnp.stack([top, total, label], 0), axis_name, perm)
        other_top, other_total, other_label = packed[0], packed[1], packed[2]
        merged = jnp.maximum(top, other_top)
        total = total * jnp.exp(top - merged) + other_total * jnp.exp(other_top - merged)
        label = label + other_label
        top = merged
        step *= 2
    return top, total, label


def gather_small(values, axis_name, size, index):
    if size & (size - 1):
        return lax.all_gather(values, axis_name, axis=0, tiled=True)
    count = values.shape[0]
    slots = jnp.zeros((size * count,), values.dtype)
    slots = lax.dynamic_update_slice_in_dim(slots, values, index * count, 0)
    step = 1
    while step < size:
        perm = [(i, i ^ step) for i in range(size)]
        slots = slots + lax.ppermute(slots, axis_name, perm)
        step *= 2
    return slots


def body(inputs, labels, phases, sign_bits, moment_first, moment_second):
    row_count, owned_blocks, doubled = inputs.shape
    block_len = doubled // 2
    blocks = phases.shape[1]
    pairs_here = sign_bits.shape[0]
    group_count = lax.axis_size("grp")
    feat_count = lax.axis_size("feat")
    total_pairs = pairs_here * group_count
    net_count = 2 * pairs_here
    own_columns = blocks // group_count
    group_index = lax.axis_index("grp")
    feat_index = lax.axis_index("feat")

    directions = (2 * sign_bits - 1).astype(jnp.bfloat16)
    all_directions = gather_by_permutes(directions, "grp", group_count, group_index)
    all_directions = all_directions.reshape((total_pairs,) + directions.shape[1:])
    moments = jnp.stack([moment_first, moment_second], 0)
    all_moments = gather_by_permutes(moments, "grp", group_count, group_index)
    all_moments = jnp.transpose(all_moments, (1, 2, 0, 3, 4)).reshape(
        (2, owned_blocks, blocks, block_len)
    )
    all_first = all_moments[0]
    all_second = all_moments[1]

    cosine, sine_part = tables(block_len)
    local_in = jnp.transpose(inputs, (1, 0, 2)).reshape(owned_blocks * row_count, doubled)
    in_real = local_in[:, :block_len]
    in_imag = local_in[:, block_len:]
    f32 = jnp.float32
    spec_real = jnp.dot(in_real, cosine, preferred_element_type=f32) + jnp.dot(
        in_imag, sine_part, preferred_element_type=f32
    )
    spec_imag = jnp.dot(in_imag, cosine, preferred_element_type=f32) - jnp.dot(
        in_real, sine_part, preferred_element_type=f32
    )
    spectra = jnp.concatenate([spec_real, spec_imag], 1).astype(jnp.bfloat16)
    spectra = spectra.reshape(owned_blocks, row_count, doubled)
    spectra_all = lax.all_gather(spectra, "feat", axis=0, tiled=True)

    angle_plus = phases + jnp.float32(perturb_size)
    angle_minus = phases - jnp.float32(perturb_size)
    cos_plus = to_bf16(jnp.cos(angle_plus))
    sin_plus = to_bf16(jnp.sin(angle_plus))
    cos_minus = to_bf16(jnp.cos(angle_minus))
    sin_minus = to_bf16(jnp.sin(angle_minus))
    up = sign_bits == 1
    t_real = jnp.stack(
        [jnp.where(up, cos_plus, cos_minus), jnp.where(up, cos_minus, cos_plus)], 1
    ).reshape(net_count, owned_blocks, blocks, block_len)
    t_imag = jnp.stack(
        [jnp.where(up, sin_plus, sin_minus), jnp.where(up, sin_minus, sin_plus)], 1
    ).reshape(net_count, owned_blocks, blocks, block_len)

    mixed = mix(spectra_all, t_real, t_imag)
    mixed = mixed.reshape(net_count * owned_blocks * row_count, doubled)
    mix_real = mixed[:, :block_len]
    mix_imag = mixed[:, block_len:]
    field_real = jnp.dot(mix_real, cosine, preferred_element_type=f32) - jnp.dot(
        mix_imag, sine_part, preferred_element_type=f32
    )
    field_imag = jnp.dot(mix_real, sine_part, preferred_element_type=f32) + jnp.dot(
        mix_imag, cosine, preferred_element_type=f32
    )
    intensity = field_real**2 + field_imag**2
    logits = logit_scale * intensity.reshape(net_count, owned_blocks, row_count, block_len)
    first_class = feat_index * (owned_blocks * block_len)
    classes = first_class + jnp.arange(owned_blocks * block_len, dtype=jnp.int32).reshape(
        owned_blocks, 1, block_len
    )
    matches = classes == labels[None, :, None]
    local_top = jnp.max(logits, axis=(1, 3))
    local_total = jnp.sum(jnp.exp(logits - local_top[:, None, :, None]), axis=(1, 3))
    local_label = jnp.sum(jnp.where(matches[None], logits, 0.0), axis=(1, 3))
    row_top, row_total, row_label = merge_stats(
        local_top, local_total, local_label, "feat", feat_count
    )
    losses = jnp.mean(row_top + jnp.log(row_total) - row_label, axis=1)
    losses = losses.reshape(pairs_here, 2)
    own_differences = (losses[:, 0] - losses[:, 1]) / (2.0 * perturb_size)
    differences = gather_small(own_differences, "grp", group_count, group_index)

    estimate_all = (
        jnp.sum(differences[:, None, None, None] * all_directions.astype(f32), axis=0)
        / total_pairs
    )
    first_bias = 1.0 - beta_first**ADAM_STEP
    second_bias = 1.0 - beta_second**ADAM_STEP
    first_all = beta_first * all_first + (1.0 - beta_first) * estimate_all
    second_all = beta_second * all_second + (1.0 - beta_second) * estimate_all * estimate_all
    phases_next = phases - learn_rate * (first_all / first_bias) / (
        jnp.sqrt(second_all / second_bias) + adam_eps
    )
    first_column = group_index * own_columns
    estimate = lax.dynamic_slice_in_dim(estimate_all, first_column, own_columns, 1)
    first_new = beta_first * moment_first + (1.0 - beta_first) * estimate
    second_new = beta_second * moment_second + (1.0 - beta_second) * estimate * estimate
    return (estimate, first_new, second_new, phases_next)


def solution(mesh):
    return jax.shard_map(
        body,
        mesh=mesh,
        in_specs=(
            P(None, "feat", None),
            P(),
            P("feat", None, None),
            P("grp", "feat", None, None),
            P("feat", "grp", None),
            P("feat", "grp", None),
        ),
        out_specs=(
            P("feat", "grp", None),
            P("feat", "grp", None),
            P("feat", "grp", None),
            P("feat", None, None),
        ),
        check_vma=False,
    )
```

```python
import functools
import math

import jax
import jax.numpy as jnp
from jax import lax
from jax.experimental import pallas as pl
from jax.experimental.pallas import tpu as pltpu
from jax.sharding import PartitionSpec as P

ADAM_STEP = 10


logit_scale = 3.0
perturb_size = 0.2
learn_rate = 0.1
beta_first = 0.9
beta_second = 0.999
adam_eps = 1e-08


def tables(block_len):
    low_len = 1 << (int(math.log2(block_len)) // 2)
    high_len = block_len // low_len
    counter = jnp.arange(block_len, dtype=jnp.int32)
    high = jnp.arange(high_len, dtype=jnp.int32) * low_len
    low = jnp.arange(low_len, dtype=jnp.int32)
    step = 2.0 * math.pi / block_len
    high_angle = (high[:, None] * counter[None, :] % block_len).astype(jnp.float32) * step
    low_angle = (low[:, None] * counter[None, :] % block_len).astype(jnp.float32) * step
    high_cos, high_sin = jnp.cos(high_angle), jnp.sin(high_angle)
    low_cos, low_sin = jnp.cos(low_angle), jnp.sin(low_angle)
    factor = 1.0 / math.sqrt(block_len)
    cosine = high_cos[:, None] * low_cos[None] - high_sin[:, None] * low_sin[None]
    sine_part = high_sin[:, None] * low_cos[None] + high_cos[:, None] * low_sin[None]
    cosine = (cosine * factor).astype(jnp.bfloat16).reshape(block_len, block_len)
    sine_part = (sine_part * factor).astype(jnp.bfloat16).reshape(block_len, block_len)
    return cosine, sine_part


def to_bf16(values):
    return lax.reduce_precision(values, exponent_bits=8, mantissa_bits=7)


def mix_kernel(s_ref, *refs, blocks, block_len, rows, chunk, factor, virtual):
    tr_refs = refs[:virtual]
    ti_refs = refs[virtual : 2 * virtual]
    o_ref, s32_ref = refs[2 * virtual :]
    half_factor = 0.5 * factor

    @pl.when(pl.program_id(0) == 0)
    def _():
        def convert(j, carry):
            s32_ref[j] = s_ref[j].astype(jnp.float32)
            return carry

        lax.fori_loop(0, blocks, convert, 0)

    for start in range(0, block_len, chunk):
        def step(j, carry):
            s_real = s32_ref[j, :, pl.ds(start, chunk)]
            s_imag = s32_ref[j, :, pl.ds(block_len + start, chunk)]
            out = []
            for v in range(virtual):
                t_real = tr_refs[v][0, pl.ds(j, 1), pl.ds(start, chunk)]
                t_imag = ti_refs[v][0, pl.ds(j, 1), pl.ds(start, chunk)]
                out.append(carry[2 * v] + (t_real * s_real - t_imag * s_imag))
                out.append(carry[2 * v + 1] + (t_real * s_imag + t_imag * s_real))
            return tuple(out)

        zero = jnp.zeros((rows, chunk), jnp.float32)
        acc = lax.fori_loop(0, blocks, step, (zero,) * (2 * virtual), unroll=2)
        for p in range(virtual - 1):
            for sense in range(2):
                sign = 1.0 if sense == 0 else -1.0
                net_real = acc[0] + sign * acc[2 + 2 * p]
                net_imag = acc[1] + sign * acc[3 + 2 * p]
                net = 2 * p + sense
                o_ref[net, 0, :, pl.ds(start, chunk)] = (net_real * half_factor).astype(o_ref.dtype)
                o_ref[net, 0, :, pl.ds(block_len + start, chunk)] = (net_imag * half_factor).astype(
                    o_ref.dtype
                )


def mix(spectra_all, t_real, t_imag):
    blocks, rows, doubled = spectra_all.shape
    block_len = doubled // 2
    virtual, owned = t_real.shape[:2]
    nets = 2 * (virtual - 1)
    kernel = functools.partial(
        mix_kernel,
        blocks=blocks,
        block_len=block_len,
        rows=rows,
        chunk=256,
        factor=1.0 / math.sqrt(blocks),
        virtual=virtual,
    )
    t_spec = pl.BlockSpec((1, blocks, block_len), lambda i: (i, 0, 0))
    parts = [t_real[v] for v in range(virtual)] + [t_imag[v] for v in range(virtual)]
    return pl.pallas_call(
        kernel,
        grid=(owned,),
        in_specs=[pl.BlockSpec((blocks, rows, doubled), lambda i: (0, 0, 0))]
        + [t_spec] * (2 * virtual),
        out_specs=pl.BlockSpec((nets, 1, rows, doubled), lambda i: (0, i, 0, 0)),
        out_shape=jax.ShapeDtypeStruct((nets, owned, rows, doubled), jnp.bfloat16),
        scratch_shapes=[pltpu.VMEM((blocks, rows, doubled), jnp.float32)],
        compiler_params=pltpu.CompilerParams(
            dimension_semantics=("arbitrary",), vmem_limit_bytes=48 * 1024 * 1024
        ),
    )(spectra_all, *parts)


def gather_by_permutes(values, axis_name, size, index):
    parts = [values] + [
        lax.ppermute(values, axis_name, [(i, (i + s) % size) for i in range(size)])
        for s in range(1, size)
    ]
    order = (index - jnp.arange(size)) % size
    return jnp.take(jnp.stack(parts, 0), order, axis=0)


def merge_stats(top, total, label, axis_name, size):
    if size & (size - 1):
        tops, totals, labels = lax.all_gather((top, total, label), axis_name)
        merged = jnp.max(tops, axis=0)
        merged_total = jnp.sum(totals * jnp.exp(tops - merged[None]), axis=0)
        return merged, merged_total, jnp.sum(labels, axis=0)
    step = 1
    while step < size:
        perm = [(i, i ^ step) for i in range(size)]
        packed = lax.ppermute(jnp.stack([top, total, label], 0), axis_name, perm)
        other_top, other_total, other_label = packed[0], packed[1], packed[2]
        merged = jnp.maximum(top, other_top)
        total = total * jnp.exp(top - merged) + other_total * jnp.exp(other_top - merged)
        label = label + other_label
        top = merged
        step *= 2
    return top, total, label


def gather_small(values, axis_name, size, index):
    if size & (size - 1):
        return lax.all_gather(values, axis_name, axis=0, tiled=True)
    count = values.shape[0]
    slots = jnp.zeros((size * count,), values.dtype)
    slots = lax.dynamic_update_slice_in_dim(slots, values, index * count, 0)
    step = 1
    while step < size:
        perm = [(i, i ^ step) for i in range(size)]
        slots = slots + lax.ppermute(slots, axis_name, perm)
        step *= 2
    return slots


def body(inputs, labels, phases, sign_bits, moment_first, moment_second):
    row_count, owned_blocks, doubled = inputs.shape
    block_len = doubled // 2
    blocks = phases.shape[1]
    pairs_here = sign_bits.shape[0]
    group_count = lax.axis_size("grp")
    feat_count = lax.axis_size("feat")
    total_pairs = pairs_here * group_count
    net_count = 2 * pairs_here
    own_columns = blocks // group_count
    group_index = lax.axis_index("grp")
    feat_index = lax.axis_index("feat")

    directions = (2 * sign_bits - 1).astype(jnp.bfloat16)
    all_directions = gather_by_permutes(directions, "grp", group_count, group_index)
    all_directions = all_directions.reshape((total_pairs,) + directions.shape[1:])
    moments = jnp.stack([moment_first, moment_second], 0)
    all_moments = gather_by_permutes(moments, "grp", group_count, group_index)
    all_moments = jnp.transpose(all_moments, (1, 2, 0, 3, 4)).reshape(
        (2, owned_blocks, blocks, block_len)
    )

    cosine, sine_part = tables(block_len)
    local_in = jnp.transpose(inputs, (1, 0, 2)).reshape(owned_blocks * row_count, doubled)
    in_real = local_in[:, :block_len]
    in_imag = local_in[:, block_len:]
    f32 = jnp.float32
    spec_real = jnp.dot(in_real, cosine, preferred_element_type=f32) + jnp.dot(
        in_imag, sine_part, preferred_element_type=f32
    )
    spec_imag = jnp.dot(in_imag, cosine, preferred_element_type=f32) - jnp.dot(
        in_real, sine_part, preferred_element_type=f32
    )
    spectra = jnp.concatenate([spec_real, spec_imag], 1).astype(jnp.bfloat16)
    spectra = spectra.reshape(owned_blocks, row_count, doubled)
    spectra_all = lax.all_gather(spectra, "feat", axis=0, tiled=True)

    angle_plus = phases + jnp.float32(perturb_size)
    angle_minus = phases - jnp.float32(perturb_size)
    cos_plus = to_bf16(jnp.cos(angle_plus))
    sin_plus = to_bf16(jnp.sin(angle_plus))
    cos_minus = to_bf16(jnp.cos(angle_minus))
    sin_minus = to_bf16(jnp.sin(angle_minus))
    up = sign_bits == 1
    cos_half = cos_plus - cos_minus
    sin_half = sin_plus - sin_minus
    t_real = jnp.concatenate(
        [(cos_plus + cos_minus)[None], jnp.where(up, cos_half, -cos_half)], 0
    )
    t_imag = jnp.concatenate(
        [(sin_plus + sin_minus)[None], jnp.where(up, sin_half, -sin_half)], 0
    )
    spectra_all, all_directions, all_moments = lax.optimization_barrier(
        (spectra_all, all_directions, all_moments)
    )

    mixed = mix(spectra_all, t_real, t_imag)
    mixed = mixed.reshape(net_count * owned_blocks * row_count, doubled)
    mix_real = mixed[:, :block_len]
    mix_imag = mixed[:, block_len:]
    field_real = jnp.dot(mix_real, cosine, preferred_element_type=f32) - jnp.dot(
        mix_imag, sine_part, preferred_element_type=f32
    )
    field_imag = jnp.dot(mix_real, sine_part, preferred_element_type=f32) + jnp.dot(
        mix_imag, cosine, preferred_element_type=f32
    )
    intensity = field_real**2 + field_imag**2
    logits = logit_scale * intensity.reshape(net_count, owned_blocks, row_count, block_len)
    first_class = feat_index * (owned_blocks * block_len)
    classes = first_class + jnp.arange(owned_blocks * block_len, dtype=jnp.int32).reshape(
        owned_blocks, 1, block_len
    )
    matches = classes == labels[None, :, None]
    local_top = jnp.max(logits, axis=(1, 3))
    local_total = jnp.sum(jnp.exp(logits - local_top[:, None, :, None]), axis=(1, 3))
    local_label = jnp.sum(jnp.where(matches[None], logits, 0.0), axis=(1, 3))
    row_top, row_total, row_label = merge_stats(
        local_top, local_total, local_label, "feat", feat_count
    )
    losses = jnp.mean(row_top + jnp.log(row_total) - row_label, axis=1)
    losses = losses.reshape(pairs_here, 2)
    own_differences = (losses[:, 0] - losses[:, 1]) / (2.0 * perturb_size)
    differences = gather_small(own_differences, "grp", group_count, group_index)

    estimate_all = (
        jnp.sum(differences[:, None, None, None] * all_directions.astype(f32), axis=0)
        / total_pairs
    )
    all_first = all_moments[0]
    all_second = all_moments[1]
    first_bias = 1.0 - beta_first**ADAM_STEP
    second_bias = 1.0 - beta_second**ADAM_STEP
    first_all = beta_first * all_first + (1.0 - beta_first) * estimate_all
    second_all = beta_second * all_second + (1.0 - beta_second) * estimate_all * estimate_all
    phases_next = phases - learn_rate * (first_all / first_bias) / (
        jnp.sqrt(second_all / second_bias) + adam_eps
    )
    first_column = group_index * own_columns
    estimate = lax.dynamic_slice_in_dim(estimate_all, first_column, own_columns, 1)
    first_new = beta_first * moment_first + (1.0 - beta_first) * estimate
    second_new = beta_second * moment_second + (1.0 - beta_second) * estimate * estimate
    return (estimate, first_new, second_new, phases_next)


def solution(mesh):
    return jax.shard_map(
        body,
        mesh=mesh,
        in_specs=(
            P(None, "feat", None),
            P(),
            P("feat", None, None),
            P("grp", "feat", None, None),
            P("feat", "grp", None),
            P("feat", "grp", None),
        ),
        out_specs=(
            P("feat", "grp", None),
            P("feat", "grp", None),
            P("feat", "grp", None),
            P("feat", None, None),
        ),
        check_vma=False,
    )
```

```python
import functools
import math

import jax
import jax.numpy as jnp
from jax import lax
from jax.experimental import pallas as pl
from jax.experimental.pallas import tpu as pltpu
from jax.sharding import PartitionSpec as P

ADAM_STEP = 10


logit_scale = 3.0
perturb_size = 0.2
learn_rate = 0.1
beta_first = 0.9
beta_second = 0.999
adam_eps = 1e-08


def tables(block_len):
    low_len = 1 << (int(math.log2(block_len)) // 2)
    high_len = block_len // low_len
    counter = jnp.arange(block_len, dtype=jnp.int32)
    high = jnp.arange(high_len, dtype=jnp.int32) * low_len
    low = jnp.arange(low_len, dtype=jnp.int32)
    step = 2.0 * math.pi / block_len
    high_angle = (high[:, None] * counter[None, :] % block_len).astype(jnp.float32) * step
    low_angle = (low[:, None] * counter[None, :] % block_len).astype(jnp.float32) * step
    high_cos, high_sin = jnp.cos(high_angle), jnp.sin(high_angle)
    low_cos, low_sin = jnp.cos(low_angle), jnp.sin(low_angle)
    factor = 1.0 / math.sqrt(block_len)
    cosine = high_cos[:, None] * low_cos[None] - high_sin[:, None] * low_sin[None]
    sine_part = high_sin[:, None] * low_cos[None] + high_cos[:, None] * low_sin[None]
    cosine = (cosine * factor).astype(jnp.bfloat16).reshape(block_len, block_len)
    sine_part = (sine_part * factor).astype(jnp.bfloat16).reshape(block_len, block_len)
    return cosine, sine_part


def to_bf16(values):
    return lax.reduce_precision(values, exponent_bits=8, mantissa_bits=7)


def mix_kernel(s_ref, *refs, blocks, block_len, rows, chunk, factor, virtual):
    tr_refs = refs[:virtual]
    ti_refs = refs[virtual : 2 * virtual]
    o_ref, s32_ref = refs[2 * virtual :]
    half_factor = 0.5 * factor

    @pl.when(pl.program_id(0) == 0)
    def _():
        def convert(j, carry):
            s32_ref[j] = s_ref[j].astype(jnp.float32)
            return carry

        lax.fori_loop(0, blocks, convert, 0)

    for start in range(0, block_len, chunk):
        def step(j, carry):
            s_real = s32_ref[j, :, pl.ds(start, chunk)]
            s_imag = s32_ref[j, :, pl.ds(block_len + start, chunk)]
            out = []
            for v in range(virtual):
                t_real = tr_refs[v][0, pl.ds(j, 1), pl.ds(start, chunk)]
                t_imag = ti_refs[v][0, pl.ds(j, 1), pl.ds(start, chunk)]
                out.append(carry[2 * v] + (t_real * s_real - t_imag * s_imag))
                out.append(carry[2 * v + 1] + (t_real * s_imag + t_imag * s_real))
            return tuple(out)

        zero = jnp.zeros((rows, chunk), jnp.float32)
        acc = lax.fori_loop(0, blocks, step, (zero,) * (2 * virtual), unroll=8)
        for p in range(virtual - 1):
            for sense in range(2):
                sign = 1.0 if sense == 0 else -1.0
                net_real = acc[0] + sign * acc[2 + 2 * p]
                net_imag = acc[1] + sign * acc[3 + 2 * p]
                net = 2 * p + sense
                o_ref[net, 0, :, pl.ds(start, chunk)] = (net_real * half_factor).astype(o_ref.dtype)
                o_ref[net, 0, :, pl.ds(block_len + start, chunk)] = (net_imag * half_factor).astype(
                    o_ref.dtype
                )


def mix(spectra_all, t_real, t_imag):
    blocks, rows, doubled = spectra_all.shape
    block_len = doubled // 2
    virtual, owned = t_real.shape[:2]
    nets = 2 * (virtual - 1)
    kernel = functools.partial(
        mix_kernel,
        blocks=blocks,
        block_len=block_len,
        rows=rows,
        chunk=256,
        factor=1.0 / math.sqrt(blocks),
        virtual=virtual,
    )
    t_spec = pl.BlockSpec((1, blocks, block_len), lambda i: (i, 0, 0))
    parts = [t_real[v] for v in range(virtual)] + [t_imag[v] for v in range(virtual)]
    return pl.pallas_call(
        kernel,
        grid=(owned,),
        in_specs=[pl.BlockSpec((blocks, rows, doubled), lambda i: (0, 0, 0))]
        + [t_spec] * (2 * virtual),
        out_specs=pl.BlockSpec((nets, 1, rows, doubled), lambda i: (0, i, 0, 0)),
        out_shape=jax.ShapeDtypeStruct((nets, owned, rows, doubled), jnp.bfloat16),
        scratch_shapes=[pltpu.VMEM((blocks, rows, doubled), jnp.float32)],
        compiler_params=pltpu.CompilerParams(
            dimension_semantics=("arbitrary",), vmem_limit_bytes=48 * 1024 * 1024
        ),
    )(spectra_all, *parts)


def gather_by_permutes(values, axis_name, size, index):
    parts = [values] + [
        lax.ppermute(values, axis_name, [(i, (i + s) % size) for i in range(size)])
        for s in range(1, size)
    ]
    order = (index - jnp.arange(size)) % size
    return jnp.take(jnp.stack(parts, 0), order, axis=0)


def merge_stats(top, total, label, axis_name, size):
    if size & (size - 1):
        tops, totals, labels = lax.all_gather((top, total, label), axis_name)
        merged = jnp.max(tops, axis=0)
        merged_total = jnp.sum(totals * jnp.exp(tops - merged[None]), axis=0)
        return merged, merged_total, jnp.sum(labels, axis=0)
    step = 1
    while step < size:
        perm = [(i, i ^ step) for i in range(size)]
        packed = lax.ppermute(jnp.stack([top, total, label], 0), axis_name, perm)
        other_top, other_total, other_label = packed[0], packed[1], packed[2]
        merged = jnp.maximum(top, other_top)
        total = total * jnp.exp(top - merged) + other_total * jnp.exp(other_top - merged)
        label = label + other_label
        top = merged
        step *= 2
    return top, total, label


def gather_small(values, axis_name, size, index):
    if size & (size - 1):
        return lax.all_gather(values, axis_name, axis=0, tiled=True)
    count = values.shape[0]
    slots = jnp.zeros((size * count,), values.dtype)
    slots = lax.dynamic_update_slice_in_dim(slots, values, index * count, 0)
    step = 1
    while step < size:
        perm = [(i, i ^ step) for i in range(size)]
        slots = slots + lax.ppermute(slots, axis_name, perm)
        step *= 2
    return slots


def body(inputs, labels, phases, sign_bits, moment_first, moment_second):
    row_count, owned_blocks, doubled = inputs.shape
    block_len = doubled // 2
    blocks = phases.shape[1]
    pairs_here = sign_bits.shape[0]
    group_count = lax.axis_size("grp")
    feat_count = lax.axis_size("feat")
    total_pairs = pairs_here * group_count
    net_count = 2 * pairs_here
    own_columns = blocks // group_count
    group_index = lax.axis_index("grp")
    feat_index = lax.axis_index("feat")

    directions = (2 * sign_bits - 1).astype(jnp.bfloat16)
    all_directions = gather_by_permutes(directions, "grp", group_count, group_index)
    all_directions = all_directions.reshape((total_pairs,) + directions.shape[1:])
    moments = jnp.stack([moment_first, moment_second], 0)
    all_moments = gather_by_permutes(moments, "grp", group_count, group_index)
    all_moments = jnp.transpose(all_moments, (1, 2, 0, 3, 4)).reshape(
        (2, owned_blocks, blocks, block_len)
    )

    cosine, sine_part = tables(block_len)
    local_in = jnp.transpose(inputs, (1, 0, 2)).reshape(owned_blocks * row_count, doubled)
    in_real = local_in[:, :block_len]
    in_imag = local_in[:, block_len:]
    f32 = jnp.float32
    spec_real = jnp.dot(in_real, cosine, preferred_element_type=f32) + jnp.dot(
        in_imag, sine_part, preferred_element_type=f32
    )
    spec_imag = jnp.dot(in_imag, cosine, preferred_element_type=f32) - jnp.dot(
        in_real, sine_part, preferred_element_type=f32
    )
    spectra = jnp.concatenate([spec_real, spec_imag], 1).astype(jnp.bfloat16)
    spectra = spectra.reshape(owned_blocks, row_count, doubled)
    spectra_all = lax.all_gather(spectra, "feat", axis=0, tiled=True)

    angle_plus = phases + jnp.float32(perturb_size)
    angle_minus = phases - jnp.float32(perturb_size)
    cos_plus = to_bf16(jnp.cos(angle_plus))
    sin_plus = to_bf16(jnp.sin(angle_plus))
    cos_minus = to_bf16(jnp.cos(angle_minus))
    sin_minus = to_bf16(jnp.sin(angle_minus))
    up = sign_bits == 1
    cos_half = cos_plus - cos_minus
    sin_half = sin_plus - sin_minus
    t_real = jnp.concatenate(
        [(cos_plus + cos_minus)[None], jnp.where(up, cos_half, -cos_half)], 0
    )
    t_imag = jnp.concatenate(
        [(sin_plus + sin_minus)[None], jnp.where(up, sin_half, -sin_half)], 0
    )
    spectra_all, all_directions, all_moments = lax.optimization_barrier(
        (spectra_all, all_directions, all_moments)
    )

    mixed = mix(spectra_all, t_real, t_imag)
    mixed = mixed.reshape(net_count * owned_blocks * row_count, doubled)
    mix_real = mixed[:, :block_len]
    mix_imag = mixed[:, block_len:]
    field_real = jnp.dot(mix_real, cosine, preferred_element_type=f32) - jnp.dot(
        mix_imag, sine_part, preferred_element_type=f32
    )
    field_imag = jnp.dot(mix_real, sine_part, preferred_element_type=f32) + jnp.dot(
        mix_imag, cosine, preferred_element_type=f32
    )
    intensity = field_real**2 + field_imag**2
    logits = logit_scale * intensity.reshape(net_count, owned_blocks, row_count, block_len)
    first_class = feat_index * (owned_blocks * block_len)
    classes = first_class + jnp.arange(owned_blocks * block_len, dtype=jnp.int32).reshape(
        owned_blocks, 1, block_len
    )
    matches = classes == labels[None, :, None]
    local_top = jnp.max(logits, axis=(1, 3))
    local_total = jnp.sum(jnp.exp(logits - local_top[:, None, :, None]), axis=(1, 3))
    local_label = jnp.sum(jnp.where(matches[None], logits, 0.0), axis=(1, 3))
    row_top, row_total, row_label = merge_stats(
        local_top, local_total, local_label, "feat", feat_count
    )
    losses = jnp.mean(row_top + jnp.log(row_total) - row_label, axis=1)
    losses = losses.reshape(pairs_here, 2)
    own_differences = (losses[:, 0] - losses[:, 1]) / (2.0 * perturb_size)
    differences = gather_small(own_differences, "grp", group_count, group_index)

    estimate_all = (
        jnp.sum(differences[:, None, None, None] * all_directions.astype(f32), axis=0)
        / total_pairs
    )
    all_first = all_moments[0]
    all_second = all_moments[1]
    first_bias = 1.0 - beta_first**ADAM_STEP
    second_bias = 1.0 - beta_second**ADAM_STEP
    first_all = beta_first * all_first + (1.0 - beta_first) * estimate_all
    second_all = beta_second * all_second + (1.0 - beta_second) * estimate_all * estimate_all
    phases_next = phases - learn_rate * (first_all / first_bias) / (
        jnp.sqrt(second_all / second_bias) + adam_eps
    )
    first_column = group_index * own_columns
    estimate = lax.dynamic_slice_in_dim(estimate_all, first_column, own_columns, 1)
    first_new = beta_first * moment_first + (1.0 - beta_first) * estimate
    second_new = beta_second * moment_second + (1.0 - beta_second) * estimate * estimate
    return (estimate, first_new, second_new, phases_next)


def solution(mesh):
    return jax.shard_map(
        body,
        mesh=mesh,
        in_specs=(
            P(None, "feat", None),
            P(),
            P("feat", None, None),
            P("grp", "feat", None, None),
            P("feat", "grp", None),
            P("feat", "grp", None),
        ),
        out_specs=(
            P("feat", "grp", None),
            P("feat", "grp", None),
            P("feat", "grp", None),
            P("feat", None, None),
        ),
        check_vma=False,
    )
```

```python
import functools
import math

import jax
import jax.numpy as jnp
from jax import lax
from jax.experimental import pallas as pl
from jax.experimental.pallas import tpu as pltpu
from jax.sharding import PartitionSpec as P

ADAM_STEP = 10


logit_scale = 3.0
perturb_size = 0.2
learn_rate = 0.1
beta_first = 0.9
beta_second = 0.999
adam_eps = 1e-08


def tables(block_len):
    low_len = 1 << (int(math.log2(block_len)) // 2)
    high_len = block_len // low_len
    counter = jnp.arange(block_len, dtype=jnp.int32)
    high = jnp.arange(high_len, dtype=jnp.int32) * low_len
    low = jnp.arange(low_len, dtype=jnp.int32)
    step = 2.0 * math.pi / block_len
    high_angle = (high[:, None] * counter[None, :] % block_len).astype(jnp.float32) * step
    low_angle = (low[:, None] * counter[None, :] % block_len).astype(jnp.float32) * step
    high_cos, high_sin = jnp.cos(high_angle), jnp.sin(high_angle)
    low_cos, low_sin = jnp.cos(low_angle), jnp.sin(low_angle)
    factor = 1.0 / math.sqrt(block_len)
    cosine = high_cos[:, None] * low_cos[None] - high_sin[:, None] * low_sin[None]
    sine_part = high_sin[:, None] * low_cos[None] + high_cos[:, None] * low_sin[None]
    cosine = (cosine * factor).astype(jnp.bfloat16).reshape(block_len, block_len)
    sine_part = (sine_part * factor).astype(jnp.bfloat16).reshape(block_len, block_len)
    return cosine, sine_part


def to_bf16(values):
    return lax.reduce_precision(values, exponent_bits=8, mantissa_bits=7)


def mix_kernel(s_ref, *refs, blocks, block_len, rows, chunk, factor, virtual):
    tr_refs = refs[:virtual]
    ti_refs = refs[virtual : 2 * virtual]
    o_ref, s32_ref = refs[2 * virtual :]
    half_factor = 0.5 * factor

    @pl.when(pl.program_id(0) == 0)
    def _():
        def convert(j, carry):
            s32_ref[j] = s_ref[j].astype(jnp.float32)
            return carry

        lax.fori_loop(0, blocks, convert, 0)

    for start in range(0, block_len, chunk):
        def step(j, carry):
            s_real = s32_ref[j, :, pl.ds(start, chunk)]
            s_imag = s32_ref[j, :, pl.ds(block_len + start, chunk)]
            out = []
            for v in range(virtual):
                t_real = tr_refs[v][0, pl.ds(j, 1), pl.ds(start, chunk)]
                t_imag = ti_refs[v][0, pl.ds(j, 1), pl.ds(start, chunk)]
                out.append(carry[2 * v] + (t_real * s_real - t_imag * s_imag))
                out.append(carry[2 * v + 1] + (t_real * s_imag + t_imag * s_real))
            return tuple(out)

        zero = jnp.zeros((rows, chunk), jnp.float32)
        acc = lax.fori_loop(0, blocks, step, (zero,) * (2 * virtual), unroll=8)
        for p in range(virtual - 1):
            for sense in range(2):
                sign = 1.0 if sense == 0 else -1.0
                net_real = acc[0] + sign * acc[2 + 2 * p]
                net_imag = acc[1] + sign * acc[3 + 2 * p]
                net = 2 * p + sense
                o_ref[net, 0, :, pl.ds(start, chunk)] = (net_real * half_factor).astype(o_ref.dtype)
                o_ref[net, 0, :, pl.ds(block_len + start, chunk)] = (net_imag * half_factor).astype(
                    o_ref.dtype
                )


def mix(spectra_all, t_real, t_imag):
    blocks, rows, doubled = spectra_all.shape
    block_len = doubled // 2
    virtual, owned = t_real.shape[:2]
    nets = 2 * (virtual - 1)
    kernel = functools.partial(
        mix_kernel,
        blocks=blocks,
        block_len=block_len,
        rows=rows,
        chunk=256,
        factor=1.0 / math.sqrt(blocks),
        virtual=virtual,
    )
    t_spec = pl.BlockSpec((1, blocks, block_len), lambda i: (i, 0, 0))
    parts = [t_real[v] for v in range(virtual)] + [t_imag[v] for v in range(virtual)]
    return pl.pallas_call(
        kernel,
        grid=(owned,),
        in_specs=[pl.BlockSpec((blocks, rows, doubled), lambda i: (0, 0, 0))]
        + [t_spec] * (2 * virtual),
        out_specs=pl.BlockSpec((nets, 1, rows, doubled), lambda i: (0, i, 0, 0)),
        out_shape=jax.ShapeDtypeStruct((nets, owned, rows, doubled), jnp.bfloat16),
        scratch_shapes=[pltpu.VMEM((blocks, rows, doubled), jnp.float32)],
        compiler_params=pltpu.CompilerParams(
            dimension_semantics=("arbitrary",), vmem_limit_bytes=48 * 1024 * 1024
        ),
    )(spectra_all, *parts)


def estimate_sum(differences, parts, size, index):
    count = parts[0].shape[0]
    diffs = differences.reshape(size, count)

    def partial(shift):
        source = (index - shift) % size
        weights = lax.dynamic_index_in_dim(diffs, source, 0, keepdims=False)
        return jnp.sum(weights[:, None, None, None] * parts[shift].astype(jnp.float32), axis=0)

    if size != 4:
        stacked = jnp.stack(parts, 0)
        ordered = jnp.take(stacked, (index - jnp.arange(size)) % size, axis=0)
        flat = ordered.reshape((size * count,) + parts[0].shape[1:])
        return jnp.sum(differences[:, None, None, None] * flat.astype(jnp.float32), axis=0)
    sums = [partial(shift) for shift in range(size)]
    even = (sums[0] + sums[3]) + (sums[1] + sums[2])
    odd = (sums[0] + sums[1]) + (sums[2] + sums[3])
    return jnp.where(index % 2 == 0, even, odd)


def permuted_parts(values, axis_name, size):
    return [values] + [
        lax.ppermute(values, axis_name, [(i, (i + s) % size) for i in range(size)])
        for s in range(1, size)
    ]


def in_source_order(parts, size, index):
    order = (index - jnp.arange(size)) % size
    return jnp.take(jnp.stack(parts, 0), order, axis=0)


def gather_by_permutes(values, axis_name, size, index):
    parts = [values] + [
        lax.ppermute(values, axis_name, [(i, (i + s) % size) for i in range(size)])
        for s in range(1, size)
    ]
    order = (index - jnp.arange(size)) % size
    return jnp.take(jnp.stack(parts, 0), order, axis=0)


def merge_stats(top, total, label, axis_name, size):
    if size & (size - 1):
        tops, totals, labels = lax.all_gather((top, total, label), axis_name)
        merged = jnp.max(tops, axis=0)
        merged_total = jnp.sum(totals * jnp.exp(tops - merged[None]), axis=0)
        return merged, merged_total, jnp.sum(labels, axis=0)
    step = 1
    while step < size:
        perm = [(i, i ^ step) for i in range(size)]
        packed = lax.ppermute(jnp.stack([top, total, label], 0), axis_name, perm)
        other_top, other_total, other_label = packed[0], packed[1], packed[2]
        merged = jnp.maximum(top, other_top)
        total = total * jnp.exp(top - merged) + other_total * jnp.exp(other_top - merged)
        label = label + other_label
        top = merged
        step *= 2
    return top, total, label


def gather_small(values, axis_name, size, index, stride=1):
    count = values.shape[0]
    slots = jnp.zeros((size * count,), values.dtype)
    slots = lax.dynamic_update_slice_in_dim(slots, values, index * count, 0)
    if size & (size - 1):
        owner = (lax.axis_index(axis_name) % stride) == 0
        return lax.psum(jnp.where(owner, slots, 0.0), axis_name)
    step = 1
    while step < size:
        perm = [(i, i ^ (step * stride)) for i in range(size * stride)]
        slots = slots + lax.ppermute(slots, axis_name, perm)
        step *= 2
    return slots


def body(inputs, labels, phases, sign_bits, moment_first, moment_second):
    row_count, owned_blocks, doubled = inputs.shape
    block_len = doubled // 2
    blocks = phases.shape[1]
    pairs_here = sign_bits.shape[0]
    group_count = lax.axis_size("grp")
    feat_count = lax.axis_size("feat")
    total_pairs = pairs_here * group_count
    net_count = 2 * pairs_here
    own_columns = blocks // group_count
    group_index = lax.axis_index("grp")
    feat_index = lax.axis_index("feat")

    directions = (2 * sign_bits - 1).astype(jnp.bfloat16)
    direction_parts = permuted_parts(directions, "grp", group_count)
    moments = jnp.stack([moment_first, moment_second], 0)
    moments = jnp.transpose(moments, (2, 0, 1, 3))
    all_moments = lax.all_gather(moments, "grp", axis=0, tiled=True)
    all_moments = jnp.transpose(all_moments, (1, 2, 0, 3)).reshape(
        (2, owned_blocks, blocks, block_len)
    )

    row_parts = 2 if group_count % 2 == 0 and row_count % 32 == 0 else 1
    rows_here = row_count // row_parts
    row_part = group_index % row_parts
    first_row = row_part * rows_here
    set_pairs = pairs_here * row_parts
    if row_parts == 2:
        neighbour = jnp.where(group_index % 2 == 0, direction_parts[-1], direction_parts[1])
        first_half = jnp.where(row_part == 0, directions, neighbour)
        second_half = jnp.where(row_part == 0, neighbour, directions)
        set_directions = jnp.concatenate([first_half, second_half], 0)
    else:
        set_directions = directions

    cosine, sine_part = tables(block_len)
    own_in = lax.dynamic_slice_in_dim(inputs, first_row, rows_here, 0)
    local_in = jnp.transpose(own_in, (1, 0, 2)).reshape(owned_blocks * rows_here, doubled)
    in_real = local_in[:, :block_len]
    in_imag = local_in[:, block_len:]
    f32 = jnp.float32
    spec_real = jnp.dot(in_real, cosine, preferred_element_type=f32) + jnp.dot(
        in_imag, sine_part, preferred_element_type=f32
    )
    spec_imag = jnp.dot(in_imag, cosine, preferred_element_type=f32) - jnp.dot(
        in_real, sine_part, preferred_element_type=f32
    )
    spectra = jnp.concatenate([spec_real, spec_imag], 1).astype(jnp.bfloat16)
    spectra = spectra.reshape(owned_blocks, rows_here, doubled)
    spectra_all = lax.all_gather(spectra, "feat", axis=0, tiled=True)

    angle_plus = phases + jnp.float32(perturb_size)
    angle_minus = phases - jnp.float32(perturb_size)
    cos_plus = to_bf16(jnp.cos(angle_plus))
    sin_plus = to_bf16(jnp.sin(angle_plus))
    cos_minus = to_bf16(jnp.cos(angle_minus))
    sin_minus = to_bf16(jnp.sin(angle_minus))
    signs = set_directions.astype(f32)
    cos_half = cos_plus - cos_minus
    sin_half = sin_plus - sin_minus
    t_real = jnp.concatenate([(cos_plus + cos_minus)[None], signs * cos_half[None]], 0)
    t_imag = jnp.concatenate([(sin_plus + sin_minus)[None], signs * sin_half[None]], 0)
    spectra_all, set_directions = lax.optimization_barrier((spectra_all, set_directions))

    mixed = mix(spectra_all, t_real, t_imag)
    set_nets = 2 * set_pairs
    mixed = mixed.reshape(set_nets * owned_blocks * rows_here, doubled)
    mix_real = mixed[:, :block_len]
    mix_imag = mixed[:, block_len:]
    field_real = jnp.dot(mix_real, cosine, preferred_element_type=f32) - jnp.dot(
        mix_imag, sine_part, preferred_element_type=f32
    )
    field_imag = jnp.dot(mix_real, sine_part, preferred_element_type=f32) + jnp.dot(
        mix_imag, cosine, preferred_element_type=f32
    )
    intensity = field_real**2 + field_imag**2
    logits = logit_scale * intensity.reshape(set_nets, owned_blocks, rows_here, block_len)
    first_class = feat_index * (owned_blocks * block_len)
    classes = first_class + jnp.arange(owned_blocks * block_len, dtype=jnp.int32).reshape(
        owned_blocks, 1, block_len
    )
    own_labels = lax.dynamic_slice_in_dim(labels, first_row, rows_here, 0)
    matches = classes == own_labels[None, :, None]
    local_top = jnp.max(logits, axis=(1, 3))
    local_total = jnp.sum(jnp.exp(logits - local_top[:, None, :, None]), axis=(1, 3))
    local_label = jnp.sum(jnp.where(matches[None], logits, 0.0), axis=(1, 3))
    row_top, row_total, row_label = merge_stats(
        local_top, local_total, local_label, "feat", feat_count
    )
    row_sums = jnp.sum(row_top + jnp.log(row_total) - row_label, axis=1)
    if row_parts == 2:
        row_sums = row_sums + lax.ppermute(
            row_sums, "grp", [(i, i ^ 1) for i in range(group_count)]
        )
    losses = (row_sums / row_count).reshape(set_pairs, 2)
    set_differences = (losses[:, 0] - losses[:, 1]) / (2.0 * perturb_size)
    differences = gather_small(
        set_differences, "grp", group_count // row_parts, group_index // row_parts, row_parts
    )

    estimate_all = (
        estimate_sum(differences, direction_parts, group_count, group_index)
        / total_pairs
    )
    all_first = all_moments[0]
    all_second = all_moments[1]
    first_bias = 1.0 - beta_first**ADAM_STEP
    second_bias = 1.0 - beta_second**ADAM_STEP
    first_all = beta_first * all_first + (1.0 - beta_first) * estimate_all
    second_all = beta_second * all_second + (1.0 - beta_second) * estimate_all * estimate_all
    phases_next = phases - learn_rate * (first_all / first_bias) / (
        jnp.sqrt(second_all / second_bias) + adam_eps
    )
    first_column = group_index * own_columns
    estimate = lax.dynamic_slice_in_dim(estimate_all, first_column, own_columns, 1)
    first_new = beta_first * moment_first + (1.0 - beta_first) * estimate
    second_new = beta_second * moment_second + (1.0 - beta_second) * estimate * estimate
    return (estimate, first_new, second_new, phases_next)


def solution(mesh):
    return jax.shard_map(
        body,
        mesh=mesh,
        in_specs=(
            P(None, "feat", None),
            P(),
            P("feat", None, None),
            P("grp", "feat", None, None),
            P("feat", "grp", None),
            P("feat", "grp", None),
        ),
        out_specs=(
            P("feat", "grp", None),
            P("feat", "grp", None),
            P("feat", "grp", None),
            P("feat", None, None),
        ),
        check_vma=False,
    )
```

```python
import functools
import math

import jax
import jax.numpy as jnp
from jax import lax
from jax.experimental import pallas as pl
from jax.experimental.pallas import tpu as pltpu
from jax.sharding import PartitionSpec as P

ADAM_STEP = 10


logit_scale = 3.0
perturb_size = 0.2
learn_rate = 0.1
beta_first = 0.9
beta_second = 0.999
adam_eps = 1e-08


def tables(block_len):
    low_len = 1 << (int(math.log2(block_len)) // 2)
    high_len = block_len // low_len
    counter = jnp.arange(block_len, dtype=jnp.int32)
    high = jnp.arange(high_len, dtype=jnp.int32) * low_len
    low = jnp.arange(low_len, dtype=jnp.int32)
    step = 2.0 * math.pi / block_len
    high_angle = (high[:, None] * counter[None, :] % block_len).astype(jnp.float32) * step
    low_angle = (low[:, None] * counter[None, :] % block_len).astype(jnp.float32) * step
    high_cos, high_sin = jnp.cos(high_angle), jnp.sin(high_angle)
    low_cos, low_sin = jnp.cos(low_angle), jnp.sin(low_angle)
    factor = 1.0 / math.sqrt(block_len)
    cosine = high_cos[:, None] * low_cos[None] - high_sin[:, None] * low_sin[None]
    sine_part = high_sin[:, None] * low_cos[None] + high_cos[:, None] * low_sin[None]
    cosine = (cosine * factor).astype(jnp.bfloat16).reshape(block_len, block_len)
    sine_part = (sine_part * factor).astype(jnp.bfloat16).reshape(block_len, block_len)
    return cosine, sine_part


def to_bf16(values):
    return lax.reduce_precision(values, exponent_bits=8, mantissa_bits=7)


def mix_kernel(s_ref, *refs, blocks, block_len, rows, chunk, factor, virtual):
    tr_refs = refs[:virtual]
    ti_refs = refs[virtual : 2 * virtual]
    o_ref, s32_ref = refs[2 * virtual :]
    half_factor = 0.5 * factor

    @pl.when(pl.program_id(0) == 0)
    def _():
        def convert(j, carry):
            s32_ref[j] = s_ref[j].astype(jnp.float32)
            return carry

        lax.fori_loop(0, blocks, convert, 0)

    for start in range(0, block_len, chunk):
        def step(j, carry):
            s_real = s32_ref[j, :, pl.ds(start, chunk)]
            s_imag = s32_ref[j, :, pl.ds(block_len + start, chunk)]
            out = []
            for v in range(virtual):
                t_real = tr_refs[v][0, pl.ds(j, 1), pl.ds(start, chunk)]
                t_imag = ti_refs[v][0, pl.ds(j, 1), pl.ds(start, chunk)]
                out.append(carry[2 * v] + (t_real * s_real - t_imag * s_imag))
                out.append(carry[2 * v + 1] + (t_real * s_imag + t_imag * s_real))
            return tuple(out)

        zero = jnp.zeros((rows, chunk), jnp.float32)
        acc = lax.fori_loop(0, blocks, step, (zero,) * (2 * virtual), unroll=8)
        for p in range(virtual - 1):
            for sense in range(2):
                sign = 1.0 if sense == 0 else -1.0
                net_real = acc[0] + sign * acc[2 + 2 * p]
                net_imag = acc[1] + sign * acc[3 + 2 * p]
                net = 2 * p + sense
                o_ref[net, 0, :, pl.ds(start, chunk)] = (net_real * half_factor).astype(o_ref.dtype)
                o_ref[net, 0, :, pl.ds(block_len + start, chunk)] = (net_imag * half_factor).astype(
                    o_ref.dtype
                )


def mix(spectra_all, t_real, t_imag):
    blocks, rows, doubled = spectra_all.shape
    block_len = doubled // 2
    virtual, owned = t_real.shape[:2]
    nets = 2 * (virtual - 1)
    kernel = functools.partial(
        mix_kernel,
        blocks=blocks,
        block_len=block_len,
        rows=rows,
        chunk=256,
        factor=1.0 / math.sqrt(blocks),
        virtual=virtual,
    )
    t_spec = pl.BlockSpec((1, blocks, block_len), lambda i: (i, 0, 0))
    parts = [t_real[v] for v in range(virtual)] + [t_imag[v] for v in range(virtual)]
    return pl.pallas_call(
        kernel,
        grid=(owned,),
        in_specs=[pl.BlockSpec((blocks, rows, doubled), lambda i: (0, 0, 0))]
        + [t_spec] * (2 * virtual),
        out_specs=pl.BlockSpec((nets, 1, rows, doubled), lambda i: (0, i, 0, 0)),
        out_shape=jax.ShapeDtypeStruct((nets, owned, rows, doubled), jnp.bfloat16),
        scratch_shapes=[pltpu.VMEM((blocks, rows, doubled), jnp.float32)],
        compiler_params=pltpu.CompilerParams(
            dimension_semantics=("arbitrary",), vmem_limit_bytes=48 * 1024 * 1024
        ),
    )(spectra_all, *parts)


def estimate_sum(differences, parts, size, index):
    count = parts[0].shape[0]
    diffs = differences.reshape(size, count)

    def partial(shift):
        source = (index - shift) % size
        weights = lax.dynamic_index_in_dim(diffs, source, 0, keepdims=False)
        return jnp.sum(weights[:, None, None, None] * parts[shift].astype(jnp.float32), axis=0)

    if size != 4:
        stacked = jnp.stack(parts, 0)
        ordered = jnp.take(stacked, (index - jnp.arange(size)) % size, axis=0)
        flat = ordered.reshape((size * count,) + parts[0].shape[1:])
        return jnp.sum(differences[:, None, None, None] * flat.astype(jnp.float32), axis=0)
    sums = [partial(shift) for shift in range(size)]
    even = (sums[0] + sums[3]) + (sums[1] + sums[2])
    odd = (sums[0] + sums[1]) + (sums[2] + sums[3])
    return jnp.where(index % 2 == 0, even, odd)


def permuted_parts(values, axis_name, size):
    return [values] + [
        lax.ppermute(values, axis_name, [(i, (i + s) % size) for i in range(size)])
        for s in range(1, size)
    ]


def in_source_order(parts, size, index):
    order = (index - jnp.arange(size)) % size
    return jnp.take(jnp.stack(parts, 0), order, axis=0)


def gather_by_permutes(values, axis_name, size, index):
    parts = [values] + [
        lax.ppermute(values, axis_name, [(i, (i + s) % size) for i in range(size)])
        for s in range(1, size)
    ]
    order = (index - jnp.arange(size)) % size
    return jnp.take(jnp.stack(parts, 0), order, axis=0)


def merge_stats(top, total, label, axis_name, size):
    if size & (size - 1):
        tops, totals, labels = lax.all_gather((top, total, label), axis_name)
        merged = jnp.max(tops, axis=0)
        merged_total = jnp.sum(totals * jnp.exp(tops - merged[None]), axis=0)
        return merged, merged_total, jnp.sum(labels, axis=0)
    step = 1
    while step < size:
        perm = [(i, i ^ step) for i in range(size)]
        packed = lax.ppermute(jnp.stack([top, total, label], 0), axis_name, perm)
        other_top, other_total, other_label = packed[0], packed[1], packed[2]
        merged = jnp.maximum(top, other_top)
        total = total * jnp.exp(top - merged) + other_total * jnp.exp(other_top - merged)
        label = label + other_label
        top = merged
        step *= 2
    return top, total, label


def gather_small(values, axis_name, size, index, stride=1):
    count = values.shape[0]
    slots = jnp.zeros((size * count,), values.dtype)
    slots = lax.dynamic_update_slice_in_dim(slots, values, index * count, 0)
    if size & (size - 1):
        owner = (lax.axis_index(axis_name) % stride) == 0
        return lax.psum(jnp.where(owner, slots, 0.0), axis_name)
    step = 1
    while step < size:
        perm = [(i, i ^ (step * stride)) for i in range(size * stride)]
        slots = slots + lax.ppermute(slots, axis_name, perm)
        step *= 2
    return slots


def body(inputs, labels, phases, sign_bits, moment_first, moment_second):
    row_count, owned_blocks, doubled = inputs.shape
    block_len = doubled // 2
    blocks = phases.shape[1]
    pairs_here = sign_bits.shape[0]
    group_count = lax.axis_size("grp")
    feat_count = lax.axis_size("feat")
    total_pairs = pairs_here * group_count
    net_count = 2 * pairs_here
    own_columns = blocks // group_count
    group_index = lax.axis_index("grp")
    feat_index = lax.axis_index("feat")

    directions = (2 * sign_bits - 1).astype(jnp.bfloat16)
    direction_parts = permuted_parts(directions, "grp", group_count)
    moments = jnp.stack([moment_first, moment_second], 0)
    moment_parts = permuted_parts(moments, "grp", group_count)

    row_parts = 2 if group_count % 2 == 0 and row_count % 32 == 0 else 1
    rows_here = row_count // row_parts
    row_part = group_index % row_parts
    first_row = row_part * rows_here
    set_pairs = pairs_here * row_parts
    if row_parts == 2:
        neighbour = jnp.where(group_index % 2 == 0, direction_parts[-1], direction_parts[1])
        first_half = jnp.where(row_part == 0, directions, neighbour)
        second_half = jnp.where(row_part == 0, neighbour, directions)
        set_directions = jnp.concatenate([first_half, second_half], 0)
    else:
        set_directions = directions

    cosine, sine_part = tables(block_len)
    own_in = lax.dynamic_slice_in_dim(inputs, first_row, rows_here, 0)
    local_in = jnp.transpose(own_in, (1, 0, 2)).reshape(owned_blocks * rows_here, doubled)
    in_real = local_in[:, :block_len]
    in_imag = local_in[:, block_len:]
    f32 = jnp.float32
    spec_real = jnp.dot(in_real, cosine, preferred_element_type=f32) + jnp.dot(
        in_imag, sine_part, preferred_element_type=f32
    )
    spec_imag = jnp.dot(in_imag, cosine, preferred_element_type=f32) - jnp.dot(
        in_real, sine_part, preferred_element_type=f32
    )
    spectra = jnp.concatenate([spec_real, spec_imag], 1).astype(jnp.bfloat16)
    spectra = spectra.reshape(owned_blocks, rows_here, doubled)
    spectra_all = lax.all_gather(spectra, "feat", axis=0, tiled=True)

    angle_plus = phases + jnp.float32(perturb_size)
    angle_minus = phases - jnp.float32(perturb_size)
    cos_plus = to_bf16(jnp.cos(angle_plus))
    sin_plus = to_bf16(jnp.sin(angle_plus))
    cos_minus = to_bf16(jnp.cos(angle_minus))
    sin_minus = to_bf16(jnp.sin(angle_minus))
    signs = set_directions.astype(f32)
    cos_half = cos_plus - cos_minus
    sin_half = sin_plus - sin_minus
    t_real = jnp.concatenate([(cos_plus + cos_minus)[None], signs * cos_half[None]], 0)
    t_imag = jnp.concatenate([(sin_plus + sin_minus)[None], signs * sin_half[None]], 0)
    spectra_all, set_directions = lax.optimization_barrier((spectra_all, set_directions))

    mixed = mix(spectra_all, t_real, t_imag)
    set_nets = 2 * set_pairs
    mixed = mixed.reshape(set_nets * owned_blocks * rows_here, doubled)
    mix_real = mixed[:, :block_len]
    mix_imag = mixed[:, block_len:]
    field_real = jnp.dot(mix_real, cosine, preferred_element_type=f32) - jnp.dot(
        mix_imag, sine_part, preferred_element_type=f32
    )
    field_imag = jnp.dot(mix_real, sine_part, preferred_element_type=f32) + jnp.dot(
        mix_imag, cosine, preferred_element_type=f32
    )
    intensity = field_real**2 + field_imag**2
    logits = logit_scale * intensity.reshape(set_nets, owned_blocks, rows_here, block_len)
    first_class = feat_index * (owned_blocks * block_len)
    classes = first_class + jnp.arange(owned_blocks * block_len, dtype=jnp.int32).reshape(
        owned_blocks, 1, block_len
    )
    own_labels = lax.dynamic_slice_in_dim(labels, first_row, rows_here, 0)
    matches = classes == own_labels[None, :, None]
    local_top = jnp.max(logits, axis=(1, 3))
    local_total = jnp.sum(jnp.exp(logits - local_top[:, None, :, None]), axis=(1, 3))
    local_label = jnp.sum(jnp.where(matches[None], logits, 0.0), axis=(1, 3))
    row_top, row_total, row_label = merge_stats(
        local_top, local_total, local_label, "feat", feat_count
    )
    row_sums = jnp.sum(row_top + jnp.log(row_total) - row_label, axis=1)
    if row_parts == 2:
        row_sums = row_sums + lax.ppermute(
            row_sums, "grp", [(i, i ^ 1) for i in range(group_count)]
        )
    losses = (row_sums / row_count).reshape(set_pairs, 2)
    set_differences = (losses[:, 0] - losses[:, 1]) / (2.0 * perturb_size)
    differences = gather_small(
        set_differences, "grp", group_count // row_parts, group_index // row_parts, row_parts
    )

    estimate_all = (
        estimate_sum(differences, direction_parts, group_count, group_index)
        / total_pairs
    )
    first_bias = 1.0 - beta_first**ADAM_STEP
    second_bias = 1.0 - beta_second**ADAM_STEP
    phases_next = phases
    for shift in range(group_count):
        column = ((group_index - shift) % group_count) * own_columns
        part_estimate = lax.dynamic_slice_in_dim(estimate_all, column, own_columns, 1)
        part_phases = lax.dynamic_slice_in_dim(phases, column, own_columns, 1)
        part_first = beta_first * moment_parts[shift][0] + (1.0 - beta_first) * part_estimate
        part_second = (
            beta_second * moment_parts[shift][1]
            + (1.0 - beta_second) * part_estimate * part_estimate
        )
        part_next = part_phases - learn_rate * (part_first / first_bias) / (
            jnp.sqrt(part_second / second_bias) + adam_eps
        )
        phases_next = lax.dynamic_update_slice_in_dim(phases_next, part_next, column, 1)
    first_column = group_index * own_columns
    estimate = lax.dynamic_slice_in_dim(estimate_all, first_column, own_columns, 1)
    first_new = beta_first * moment_first + (1.0 - beta_first) * estimate
    second_new = beta_second * moment_second + (1.0 - beta_second) * estimate * estimate
    return (estimate, first_new, second_new, phases_next)


def solution(mesh):
    return jax.shard_map(
        body,
        mesh=mesh,
        in_specs=(
            P(None, "feat", None),
            P(),
            P("feat", None, None),
            P("grp", "feat", None, None),
            P("feat", "grp", None),
            P("feat", "grp", None),
        ),
        out_specs=(
            P("feat", "grp", None),
            P("feat", "grp", None),
            P("feat", "grp", None),
            P("feat", None, None),
        ),
        check_vma=False,
    )
```
